32 devices in a mesh: blk: 8 (over z, core), help: 4 (over y, x).
Axes of the slice: x: 2, y: 2, z: 4, core: 2. Of those that a mesh axis runs over, the one named last changes fastest.
Arguments:
- vectors: float32 [8, 16384], P(None, ('blk', 'help')), may hold values from -6 to 6
- tile_blocks: float32 [32, 5, 3, 256, 256], P(('blk', 'help')), may hold values from -0.1875 to 0.1875
- tile_row: int32 [32, 5, 3], P(('blk', 'help')), may hold values from 0 to 7
- tile_col: int32 [32, 5, 3], P(('blk', 'help')), may hold values from 0 to 7
- counts: int32 [32, 5], P(('blk', 'help')), may hold values from 1 to 3, as said below
Outputs:
- product: float32 [8, 16384], P(None, ('blk', 'help'))
- gram_energy: float32 [8, 8], replicated
- gram_correlation: float32 [8, 8], replicated
The draws below stay inside these ranges and needn't reach their ends.
Inputs may be any that keep to these rules, and one draw needn't show every extreme that they name: `counts`: in every group of 4 helpers one helper has 3 live slots for every band offset; every other helper has fewer, and at least one, for each offset.
All inputs are finite; a program needn't handle non-finite values.
Results may differ from the reference program's by a relative error of at most 0.0003.
Values sent between devices are 32-bit elements; how exact they have to be, the bound alone decides.
No kernel may reach another device: no remote copies, remote signals or barrier semaphores. Data moves between devices by JAX's collectives and lax.ppermute only.
A program may use at most 64 MiB of HBM per device.

```python
import jax
import jax.numpy as jnp
from jax import lax

VEC = 8
TILE = 256
BAND = 2
SLOTS = 3
NOFF = 5
GROUPS = 8
HELPERS = 4
DEVS = 32
ROWS_GRP = 8
NBASIS = 16384


def draw_counts(key, part):
    heavy_helper = jax.random.randint(jax.random.fold_in(key, 11), (GROUPS, 1, 1), 0, HELPERS)
    light_load = jax.random.randint(jax.random.fold_in(key, 12), (GROUPS, HELPERS, NOFF), 1, SLOTS)
    helper_ids = jnp.arange(HELPERS, dtype=jnp.int32)[None, :, None]
    filled = jnp.where(helper_ids == heavy_helper, SLOTS, light_load)
    return filled.reshape(DEVS, NOFF).astype(jnp.int32)


def place_ends(array, rng, smallest, largest):
    dims = array.shape
    place = [jax.random.randint(jax.random.fold_in(rng, axis), (), 0, dims[axis]) for axis in range(len(dims))]
    array = array.at[tuple(place)].set(smallest)
    longest = dims.index(max(dims))
    place[longest] = (place[longest] + 1) % dims[longest]
    return array.at[tuple(place)].set(largest)


def steps_of(rng, shape, split, smallest, top_value):
    factor_of = 1.0
    for position, parts in split:
        draws = jax.random.uniform(jax.random.fold_in(jax.random.fold_in(rng, 6), position), (parts,), jnp.float32, smallest / len(split), top_value / len(split))
        factor_of = factor_of * jnp.repeat(jnp.exp(draws), shape[position] // parts).reshape((-1,) + (1,) * (len(shape) - 1 - position))
    return factor_of


def scatter_about(key, extent, scale, most, cuts=(), held_as=jnp.bfloat16):
    loudness = steps_of(key, extent, cuts, -0.22, 0.18) if cuts else 1.0
    entries = jax.random.normal(key, extent, jnp.float32) * scale * loudness
    return jnp.minimum(jnp.maximum(entries, -most), most).astype(held_as)


def setup_inputs(seed: int = 0) -> dict:
    streams_of = jax.random.split(jax.random.key(seed), 6)
    return {
        "vectors": scatter_about(streams_of[0], (VEC, NBASIS), 1.0, 6.0, ((1, 32),), jnp.float32),
        "tile_blocks": scatter_about(streams_of[1], (DEVS, NOFF, SLOTS, TILE, TILE), (4 * TILE) ** -0.5, 0.1875, ((0, 32),), jnp.float32),
        "tile_row": place_ends(jax.random.randint(streams_of[2], (DEVS, NOFF, SLOTS), 0, ROWS_GRP), jax.random.fold_in(streams_of[2], 1), 0, ROWS_GRP - 1).astype(jnp.int32),
        "tile_col": place_ends(jax.random.randint(streams_of[3], (DEVS, NOFF, SLOTS), 0, ROWS_GRP), jax.random.fold_in(streams_of[3], 1), 0, ROWS_GRP - 1).astype(jnp.int32),
        "counts": draw_counts(jax.random.fold_in(streams_of[5], 71), 0),
    }


def reference(vectors, tile_blocks, tile_row, tile_col, counts):
    vec_tiles = vectors.reshape(VEC, NBASIS // TILE, TILE)
    slot_ids = jnp.arange(SLOTS, dtype=jnp.int32)
    row_ids = jnp.arange(ROWS_GRP, dtype=jnp.int32)

    def one_device(device):
        group_index = device // HELPERS
        partial_value = jnp.zeros((VEC, ROWS_GRP, TILE), jnp.float32)
        for offset_index in range(NOFF):
            column_block = group_index + offset_index - BAND
            valid = (column_block >= 0) & (column_block < GROUPS)
            clipped = jnp.clip(column_block, 0, GROUPS - 1)
            column_ids = (clipped * ROWS_GRP + tile_col[device, offset_index]).astype(jnp.int32)
            pieces = jnp.take(vec_tiles, column_ids, axis=1)
            live = ((slot_ids < counts[device, offset_index]) & valid).astype(jnp.float32)
            contribution = jnp.einsum("ist,stu->isu", pieces, tile_blocks[device, offset_index], precision=lax.Precision.HIGHEST)
            one_hot = (tile_row[device, offset_index][:, None] == row_ids[None, :]).astype(jnp.float32) * live[:, None]
            partial_value = partial_value + jnp.einsum("isu,sr->iru", contribution, one_hot, precision=lax.Precision.HIGHEST)
        return partial_value

    partials = lax.map(one_device, jnp.arange(DEVS, dtype=jnp.int32))
    summed = partials.reshape(GROUPS, HELPERS, VEC, ROWS_GRP, TILE).sum(axis=1)
    product = summed.transpose(1, 0, 2, 3).reshape(VEC, NBASIS)
    gram_energy = jnp.dot(vectors, product.T, precision=lax.Precision.HIGHEST, preferred_element_type=jnp.float32) / NBASIS
    gram_correlation = jnp.dot(vectors, vectors.T, precision=lax.Precision.HIGHEST, preferred_element_type=jnp.float32) / NBASIS
    return (product, gram_energy, gram_correlation)
```

```python
import jax
import jax.numpy as jnp
from jax import lax
from jax.sharding import PartitionSpec as P

VEC = 8
TILE = 256
BAND = 2
SLOTS = 3
NOFF = 5
GRAM_PAD = 128


def shifted(value, axis, steps):
    count = lax.axis_size(axis)
    initial, last = (max(0, -steps), min(count, count - steps))
    return lax.ppermute(value, axis, [(source, source + steps) for source in range(initial, last)])


def is_power_of_two(count):
    return count & (count - 1) == 0


def exchanged(value, axis, mask):
    count = lax.axis_size(axis)
    return lax.ppermute(value, axis, [(source, source ^ mask) for source in range(count)])


def gather_help(piece):
    count = lax.axis_size("help")
    if not is_power_of_two(count):
        return lax.all_gather(piece, "help", axis=1, tiled=True)
    index = lax.axis_index("help")
    held = piece
    mask = 1
    while mask < count:
        other = exchanged(held, "help", mask)
        upper = (index // mask) % 2 == 1
        held = jnp.where(
            upper, jnp.concatenate([other, held], axis=1), jnp.concatenate([held, other], axis=1)
        )
        mask *= 2
    return held


def reduce_help(partial, gram):
    count = lax.axis_size("help")
    if not is_power_of_two(count):
        return (
            lax.psum_scatter(partial, "help", scatter_dimension=1, tiled=True),
            lax.psum(gram, "help"),
        )
    index = lax.axis_index("help")
    held = partial
    mask = count // 2
    while mask >= 1:
        half = held.shape[1] // 2
        lower, upper = held[:, :half], held[:, half:]
        high = (index // mask) % 2 == 1
        keep = jnp.where(high, upper, lower)
        send = jnp.where(high, lower, upper)
        arrived = exchanged(jnp.concatenate([send, gram], axis=1), "help", mask)
        held = keep + arrived[:, :half]
        gram = gram + arrived[:, half:]
        mask //= 2
    return held, gram


def reduce_blk(gram):
    count = lax.axis_size("blk")
    if not is_power_of_two(count):
        return lax.psum(gram, "blk")
    mask = 1
    while mask < count:
        gram = gram + exchanged(gram, "blk", mask)
        mask *= 2
    return gram


def neighbour_panels(source):
    lowers = []
    uppers = []
    current = source
    for hop_index in range(BAND):
        current = shifted(current, "blk", 1)
        lowers.append(current)
    current = source
    for hop_index in range(BAND):
        current = shifted(current, "blk", -1)
        uppers.append(current)
    return lowers[::-1] + [source] + uppers


def local(vectors, tile_blocks, tile_row, tile_col, counts):
    groups = lax.axis_size("blk")
    piece_width = vectors.shape[1]
    group_width = piece_width * lax.axis_size("help")
    group_rows = group_width // TILE
    full_panel = gather_help(vectors)
    panels = neighbour_panels(full_panel)
    slot_ids = jnp.arange(SLOTS, dtype=jnp.int32)
    row_ids = jnp.arange(group_rows, dtype=jnp.int32)
    partial_value = jnp.zeros((VEC, group_rows, TILE), jnp.float32)
    for offset_index in range(NOFF):
        panel_tiles = panels[offset_index].reshape(VEC, group_rows, TILE)
        pieces = jnp.take(panel_tiles, tile_col[0, offset_index], axis=1)
        live = (slot_ids < counts[0, offset_index]).astype(jnp.float32)
        contribution = jnp.einsum(
            "ist,stu->isu", pieces, tile_blocks[0, offset_index], precision=lax.Precision.HIGHEST
        )
        one_hot = (tile_row[0, offset_index][:, None] == row_ids[None, :]).astype(
            jnp.float32
        ) * live[:, None]
        partial_value = partial_value + jnp.einsum(
            "isu,sr->iru", contribution, one_hot, precision=lax.Precision.HIGHEST
        )
    flattened = partial_value.reshape(VEC, group_width)
    basis_size = float(groups * group_width)
    correlation_term = jnp.dot(
        vectors, vectors.T, precision=lax.Precision.HIGHEST, preferred_element_type=jnp.float32
    )
    energy_term = jnp.dot(
        full_panel, flattened.T, precision=lax.Precision.HIGHEST, preferred_element_type=jnp.float32
    )
    gram = jnp.zeros((VEC, GRAM_PAD), jnp.float32)
    gram = gram.at[:, :VEC].set(energy_term).at[:, VEC : 2 * VEC].set(correlation_term)
    product, gram = reduce_help(flattened, gram)
    gram = reduce_blk(gram)
    gram = gram / basis_size
    return (product, gram[:, :VEC], gram[:, VEC : 2 * VEC])


def solution(mesh):
    placed = (
        P(None, ("blk", "help")),
        P(("blk", "help"), None, None, None, None),
        P(("blk", "help"), None, None),
        P(("blk", "help"), None, None),
        P(("blk", "help"), None),
    )
    return jax.shard_map(
        local,
        mesh=mesh,
        in_specs=placed,
        out_specs=(P(None, ("blk", "help")), P(), P()),
        check_vma=False,
    )
```

```python
import jax
import jax.numpy as jnp
from jax import lax
from jax.sharding import PartitionSpec as P

VEC = 8
TILE = 256
BAND = 2
SLOTS = 3
NOFF = 5
GRAM_PAD = 128


def shifted(value, axis, steps):
    count = lax.axis_size(axis)
    initial, last = (max(0, -steps), min(count, count - steps))
    return lax.ppermute(value, axis, [(source, source + steps) for source in range(initial, last)])


def is_power_of_two(count):
    return count & (count - 1) == 0


def exchanged(value, axis, mask):
    count = lax.axis_size(axis)
    return lax.ppermute(value, axis, [(source, source ^ mask) for source in range(count)])


def gather_help(piece):
    count = lax.axis_size("help")
    if not is_power_of_two(count):
        return lax.all_gather(piece, "help", axis=1, tiled=True)
    index = lax.axis_index("help")
    held = piece
    mask = 1
    while mask < count:
        other = exchanged(held, "help", mask)
        upper = (index // mask) % 2 == 1
        held = jnp.where(
            upper, jnp.concatenate([other, held], axis=1), jnp.concatenate([held, other], axis=1)
        )
        mask *= 2
    return held


def reduce_help(partial, gram):
    count = lax.axis_size("help")
    if not is_power_of_two(count):
        return (
            lax.psum_scatter(partial, "help", scatter_dimension=1, tiled=True),
            lax.psum(gram, "help"),
        )
    index = lax.axis_index("help")
    held = partial
    mask = count // 2
    while mask >= 1:
        half = held.shape[1] // 2
        lower, upper = held[:, :half], held[:, half:]
        high = (index // mask) % 2 == 1
        keep = jnp.where(high, upper, lower)
        send = jnp.where(high, lower, upper)
        arrived = exchanged(jnp.concatenate([send, gram], axis=1), "help", mask)
        held = keep + arrived[:, :half]
        gram = gram + arrived[:, half:]
        mask //= 2
    return held, gram


def reduce_blk(gram):
    count = lax.axis_size("blk")
    if not is_power_of_two(count):
        return lax.psum(gram, "blk")
    mask = 1
    while mask < count:
        gram = gram + exchanged(gram, "blk", mask)
        mask *= 2
    return gram


def neighbour_panels(source):
    lowers = []
    uppers = []
    current = source
    for hop_index in range(BAND):
        current = shifted(current, "blk", 1)
        lowers.append(current)
    current = source
    for hop_index in range(BAND):
        current = shifted(current, "blk", -1)
        uppers.append(current)
    return lowers[::-1] + [source] + uppers


def local(vectors, tile_blocks, tile_row, tile_col, counts):
    groups = lax.axis_size("blk")
    piece_width = vectors.shape[1]
    group_width = piece_width * lax.axis_size("help")
    group_rows = group_width // TILE
    full_panel = gather_help(vectors)
    panels = neighbour_panels(full_panel)
    stacked = jnp.stack(panels).reshape(NOFF, VEC, group_rows, TILE).transpose(0, 2, 1, 3)
    offset_ids = jnp.arange(NOFF, dtype=jnp.int32)[:, None]
    pieces = stacked[offset_ids, tile_col[0]]
    contribution = jnp.einsum(
        "osit,ostu->osiu", pieces, tile_blocks[0], precision=lax.Precision.HIGHEST
    )
    slot_ids = jnp.arange(SLOTS, dtype=jnp.int32)[None, :]
    row_ids = jnp.arange(group_rows, dtype=jnp.int32)
    live = (slot_ids < counts[0][:, None]).astype(jnp.float32)
    one_hot = (tile_row[0][:, :, None] == row_ids).astype(jnp.float32) * live[:, :, None]
    partial_value = jnp.einsum(
        "osiu,osr->iru", contribution, one_hot, precision=lax.Precision.HIGHEST
    )
    flattened = partial_value.reshape(VEC, group_width)
    basis_size = float(groups * group_width)
    correlation_term = jnp.dot(
        vectors, vectors.T, precision=lax.Precision.HIGHEST, preferred_element_type=jnp.float32
    )
    energy_term = jnp.dot(
        full_panel, flattened.T, precision=lax.Precision.HIGHEST, preferred_element_type=jnp.float32
    )
    gram = jnp.zeros((VEC, GRAM_PAD), jnp.float32)
    gram = gram.at[:, :VEC].set(energy_term).at[:, VEC : 2 * VEC].set(correlation_term)
    product, gram = reduce_help(flattened, gram)
    gram = reduce_blk(gram)
    gram = gram / basis_size
    return (product, gram[:, :VEC], gram[:, VEC : 2 * VEC])


def solution(mesh):
    placed = (
        P(None, ("blk", "help")),
        P(("blk", "help"), None, None, None, None),
        P(("blk", "help"), None, None),
        P(("blk", "help"), None, None),
        P(("blk", "help"), None),
    )
    return jax.shard_map(
        local,
        mesh=mesh,
        in_specs=placed,
        out_specs=(P(None, ("blk", "help")), P(), P()),
        check_vma=False,
    )
```

```python
import jax
import jax.numpy as jnp
from jax import lax
from jax.sharding import PartitionSpec as P

VEC = 8
TILE = 256
BAND = 2
SLOTS = 3
NOFF = 5
GRAM_PAD = 128


def shifted(value, axis, steps):
    count = lax.axis_size(axis)
    initial, last = (max(0, -steps), min(count, count - steps))
    return lax.ppermute(value, axis, [(source, source + steps) for source in range(initial, last)])


def is_power_of_two(count):
    return count & (count - 1) == 0


def exchanged(value, axis, mask):
    count = lax.axis_size(axis)
    return lax.ppermute(value, axis, [(source, source ^ mask) for source in range(count)])


def help_order():
    count = lax.axis_size("help")
    if not is_power_of_two(count):
        return jnp.int32(0)
    return lax.axis_index("help").astype(jnp.int32)


def gather_help(piece):
    count = lax.axis_size("help")
    if not is_power_of_two(count):
        return lax.all_gather(piece, "help", axis=1, tiled=True)
    held = piece
    mask = 1
    while mask < count:
        held = jnp.concatenate([held, exchanged(held, "help", mask)], axis=1)
        mask *= 2
    return held


def reduce_help(partial, gram):
    count = lax.axis_size("help")
    if not is_power_of_two(count):
        return (
            lax.psum_scatter(partial, "help", scatter_dimension=1, tiled=True),
            lax.psum(gram, "help"),
        )
    held = partial
    mask = count // 2
    while mask >= 1:
        half = held.shape[1] // 2
        arrived = exchanged(jnp.concatenate([held[:, half:], gram], axis=1), "help", mask)
        held = held[:, :half] + arrived[:, :half]
        gram = gram + arrived[:, half:]
        mask //= 2
    return held, gram


def reduce_blk(gram):
    count = lax.axis_size("blk")
    if not is_power_of_two(count):
        return lax.psum(gram, "blk")
    mask = 1
    while mask < count:
        gram = gram + exchanged(gram, "blk", mask)
        mask *= 2
    return gram


def neighbour_panels(source):
    lowers = []
    uppers = []
    current = source
    for hop_index in range(BAND):
        current = shifted(current, "blk", 1)
        lowers.append(current)
    current = source
    for hop_index in range(BAND):
        current = shifted(current, "blk", -1)
        uppers.append(current)
    return lowers[::-1] + [source] + uppers


def local(vectors, tile_blocks, tile_row, tile_col, counts):
    groups = lax.axis_size("blk")
    piece_width = vectors.shape[1]
    group_width = piece_width * lax.axis_size("help")
    group_rows = group_width // TILE
    full_panel = gather_help(vectors)
    panels = neighbour_panels(full_panel)
    tiles_per_piece = piece_width // TILE
    order = help_order()

    def placed(tile_index):
        return ((tile_index // tiles_per_piece) ^ order) * tiles_per_piece + tile_index % tiles_per_piece

    column_place = placed(tile_col[0])
    row_place = placed(tile_row[0])
    slot_ids = jnp.arange(SLOTS, dtype=jnp.int32)[None, :]
    row_ids = jnp.arange(group_rows, dtype=jnp.int32)
    live = (slot_ids < counts[0][:, None]).astype(jnp.float32)
    one_hot = (row_place[:, :, None] == row_ids).astype(jnp.float32) * live[:, :, None]
    partial_value = None
    for batch in ((BAND,), (BAND - 1, BAND + 1), (0, NOFF - 1)):
        chosen = jnp.array(batch, dtype=jnp.int32)
        stacked = jnp.stack([panels[o] for o in batch]).reshape(len(batch), VEC, group_rows, TILE)
        stacked = stacked.transpose(0, 2, 1, 3)
        pieces = stacked[jnp.arange(len(batch))[:, None], column_place[chosen]]
        contribution = jnp.einsum(
            "osit,ostu->osiu", pieces, tile_blocks[0, chosen], precision=lax.Precision.HIGHEST
        )
        batch_value = jnp.einsum(
            "osiu,osr->iru", contribution, one_hot[chosen], precision=lax.Precision.HIGHEST
        )
        partial_value = batch_value if partial_value is None else partial_value + batch_value
    flattened = partial_value.reshape(VEC, group_width)
    basis_size = float(groups * group_width)
    correlation_term = jnp.dot(
        vectors, vectors.T, precision=lax.Precision.HIGHEST, preferred_element_type=jnp.float32
    )
    energy_term = jnp.dot(
        full_panel, flattened.T, precision=lax.Precision.HIGHEST, preferred_element_type=jnp.float32
    )
    gram = jnp.concatenate(
        [energy_term, correlation_term, jnp.zeros((VEC, GRAM_PAD - 2 * VEC), jnp.float32)], axis=1
    )
    product, gram = reduce_help(flattened, gram)
    gram = reduce_blk(gram)
    gram = gram / basis_size
    return (product, gram[:, :VEC], gram[:, VEC : 2 * VEC])


def solution(mesh):
    placed = (
        P(None, ("blk", "help")),
        P(("blk", "help"), None, None, None, None),
        P(("blk", "help"), None, None),
        P(("blk", "help"), None, None),
        P(("blk", "help"), None),
    )
    return jax.shard_map(
        local,
        mesh=mesh,
        in_specs=placed,
        out_specs=(P(None, ("blk", "help")), P(), P()),
        check_vma=False,
    )
```

```python
import jax
import jax.numpy as jnp
from jax import lax
from jax.sharding import PartitionSpec as P

VEC = 8
TILE = 256
BAND = 2
SLOTS = 3
NOFF = 5
GRAM_PAD = 128


def shifted(value, axis, steps):
    count = lax.axis_size(axis)
    initial, last = (max(0, -steps), min(count, count - steps))
    return lax.ppermute(value, axis, [(source, source + steps) for source in range(initial, last)])


def is_power_of_two(count):
    return count & (count - 1) == 0


def exchanged(value, axis, mask):
    count = lax.axis_size(axis)
    return lax.ppermute(value, axis, [(source, source ^ mask) for source in range(count)])


def help_order():
    count = lax.axis_size("help")
    if not is_power_of_two(count):
        return jnp.int32(0)
    return lax.axis_index("help").astype(jnp.int32)


def gather_help(piece):
    count = lax.axis_size("help")
    if not is_power_of_two(count):
        return lax.all_gather(piece, "help", axis=1, tiled=True)
    held = piece
    mask = 1
    while mask < count:
        held = jnp.concatenate([held, exchanged(held, "help", mask)], axis=1)
        mask *= 2
    return held


def reduce_help(partial, gram):
    count = lax.axis_size("help")
    if not is_power_of_two(count):
        return (
            lax.psum_scatter(partial, "help", scatter_dimension=1, tiled=True),
            lax.psum(gram, "help"),
        )
    held = partial
    mask = count // 2
    while mask >= 1:
        half = held.shape[1] // 2
        arrived = exchanged(jnp.concatenate([held[:, half:], gram], axis=1), "help", mask)
        held = held[:, :half] + arrived[:, :half]
        gram = gram + arrived[:, half:]
        mask //= 2
    return held, gram


def reduce_blk(gram):
    count = lax.axis_size("blk")
    if not is_power_of_two(count):
        return lax.psum(gram, "blk")
    mask = 1
    while mask < count:
        gram = gram + exchanged(gram, "blk", mask)
        mask *= 2
    return gram


def neighbour_panels(source):
    lowers = []
    uppers = []
    current = source
    for hop_index in range(BAND):
        current = shifted(current, "blk", 1)
        lowers.append(current)
    current = source
    for hop_index in range(BAND):
        current = shifted(current, "blk", -1)
        uppers.append(current)
    return lowers[::-1] + [source] + uppers


def local(vectors, tile_blocks, tile_row, tile_col, counts):
    groups = lax.axis_size("blk")
    piece_width = vectors.shape[1]
    group_width = piece_width * lax.axis_size("help")
    group_rows = group_width // TILE
    full_panel = gather_help(vectors)
    panels = neighbour_panels(full_panel)
    tiles_per_piece = piece_width // TILE
    order = help_order()

    def placed(tile_index):
        return ((tile_index // tiles_per_piece) ^ order) * tiles_per_piece + tile_index % tiles_per_piece

    column_place = placed(tile_col[0])
    row_place = placed(tile_row[0])
    slot_ids = jnp.arange(SLOTS, dtype=jnp.int32)[None, :]
    row_ids = jnp.arange(group_rows, dtype=jnp.int32)
    live = (slot_ids < counts[0][:, None]).astype(jnp.float32)
    one_hot = (row_place[:, :, None] == row_ids).astype(jnp.float32) * live[:, :, None]
    partial_value = None
    for first, last, step in ((BAND - 1, BAND + 2, 1), (0, NOFF, NOFF - 1)):
        batch = list(range(first, last, step))
        stacked = jnp.stack([panels[o] for o in batch]).reshape(len(batch), VEC, group_rows, TILE)
        stacked = stacked.transpose(0, 2, 1, 3)
        pieces = stacked[jnp.arange(len(batch))[:, None], column_place[first:last:step]]
        contribution = jnp.einsum(
            "osit,ostu->osiu",
            pieces,
            tile_blocks[0, first:last:step],
            precision=lax.Precision.HIGHEST,
        )
        batch_value = jnp.einsum(
            "osiu,osr->iru",
            contribution,
            one_hot[first:last:step],
            precision=lax.Precision.HIGHEST,
        )
        partial_value = batch_value if partial_value is None else partial_value + batch_value
    flattened = partial_value.reshape(VEC, group_width)
    basis_size = float(groups * group_width)
    correlation_term = jnp.dot(
        vectors, vectors.T, precision=lax.Precision.HIGHEST, preferred_element_type=jnp.float32
    )
    energy_term = jnp.dot(
        full_panel, flattened.T, precision=lax.Precision.HIGHEST, preferred_element_type=jnp.float32
    )
    gram = jnp.concatenate(
        [energy_term, correlation_term, jnp.zeros((VEC, GRAM_PAD - 2 * VEC), jnp.float32)], axis=1
    )
    product, gram = reduce_help(flattened, gram)
    gram = reduce_blk(gram)
    gram = gram / basis_size
    return (product, gram[:, :VEC], gram[:, VEC : 2 * VEC])


def solution(mesh):
    placed = (
        P(None, ("blk", "help")),
        P(("blk", "help"), None, None, None, None),
        P(("blk", "help"), None, None),
        P(("blk", "help"), None, None),
        P(("blk", "help"), None),
    )
    return jax.shard_map(
        local,
        mesh=mesh,
        in_specs=placed,
        out_specs=(P(None, ("blk", "help")), P(), P()),
        check_vma=False,
    )
```

```python
import jax
import jax.numpy as jnp
from jax import lax
from jax.sharding import PartitionSpec as P

VEC = 8
TILE = 256
BAND = 2
SLOTS = 3
NOFF = 5
GRAM_PAD = 128


def shifted(value, axis, steps):
    count = lax.axis_size(axis)
    initial, last = (max(0, -steps), min(count, count - steps))
    return lax.ppermute(value, axis, [(source, source + steps) for source in range(initial, last)])


def is_power_of_two(count):
    return count & (count - 1) == 0


def exchanged(value, axis, mask):
    count = lax.axis_size(axis)
    return lax.ppermute(value, axis, [(source, source ^ mask) for source in range(count)])


def help_order():
    count = lax.axis_size("help")
    if not is_power_of_two(count):
        return jnp.int32(0)
    return lax.axis_index("help").astype(jnp.int32)


def gather_help(piece):
    count = lax.axis_size("help")
    if not is_power_of_two(count):
        return lax.all_gather(piece, "help", axis=1, tiled=True)
    held = piece
    mask = 1
    while mask < count:
        held = jnp.concatenate([held, exchanged(held, "help", mask)], axis=1)
        mask *= 2
    return held


def reduce_help(partial, gram):
    count = lax.axis_size("help")
    if not is_power_of_two(count):
        return (
            lax.psum_scatter(partial, "help", scatter_dimension=1, tiled=True),
            lax.psum(gram, "help"),
        )
    held = partial
    mask = count // 2
    while mask >= 1:
        half = held.shape[1] // 2
        arrived = exchanged(jnp.concatenate([held[:, half:], gram], axis=1), "help", mask)
        held = held[:, :half] + arrived[:, :half]
        gram = gram + arrived[:, half:]
        mask //= 2
    return held, gram


def reduce_blk(gram):
    count = lax.axis_size("blk")
    if not is_power_of_two(count):
        return lax.psum(gram, "blk")
    mask = 1
    while mask < count:
        gram = gram + exchanged(gram, "blk", mask)
        mask *= 2
    return gram


def neighbour_panels(source):
    lowers = []
    uppers = []
    current = source
    for hop_index in range(BAND):
        current = shifted(current, "blk", 1)
        lowers.append(current)
    current = source
    for hop_index in range(BAND):
        current = shifted(current, "blk", -1)
        uppers.append(current)
    return lowers[::-1] + [source] + uppers


def local(vectors, tile_blocks, tile_row, tile_col, counts):
    groups = lax.axis_size("blk")
    piece_width = vectors.shape[1]
    group_width = piece_width * lax.axis_size("help")
    group_rows = group_width // TILE
    full_panel = gather_help(vectors)
    panels = neighbour_panels(full_panel)
    tiles_per_piece = piece_width // TILE
    order = help_order()

    def placed(tile_index):
        return ((tile_index // tiles_per_piece) ^ order) * tiles_per_piece + tile_index % tiles_per_piece

    column_place = placed(tile_col[0])
    row_place = placed(tile_row[0])
    slot_ids = jnp.arange(SLOTS, dtype=jnp.int32)[None, :]
    row_ids = jnp.arange(group_rows, dtype=jnp.int32)
    live = (slot_ids < counts[0][:, None]).astype(jnp.float32)
    one_hot = (row_place[:, :, None] == row_ids).astype(jnp.float32) * live[:, :, None]
    partial_value = None
    for first, last, step in ((BAND - 1, BAND + 2, 1), (0, NOFF, NOFF - 1)):
        batch = list(range(first, last, step))
        stacked = jnp.stack([panels[o] for o in batch]).reshape(len(batch), VEC, group_rows, TILE)
        stacked = stacked.transpose(0, 2, 1, 3)
        pieces = stacked[jnp.arange(len(batch))[:, None], column_place[first:last:step]]
        contribution = jnp.einsum(
            "osit,ostu->osiu",
            pieces,
            tile_blocks[0, first:last:step],
            precision=lax.Precision.HIGH,
        )
        batch_value = jnp.einsum(
            "osiu,osr->iru",
            contribution,
            one_hot[first:last:step],
            precision=lax.Precision.HIGHEST,
        )
        partial_value = batch_value if partial_value is None else partial_value + batch_value
    flattened = partial_value.reshape(VEC, group_width)
    basis_size = float(groups * group_width)
    correlation_term = jnp.dot(
        vectors, vectors.T, precision=lax.Precision.HIGHEST, preferred_element_type=jnp.float32
    )
    energy_term = jnp.dot(
        full_panel, flattened.T, precision=lax.Precision.HIGHEST, preferred_element_type=jnp.float32
    )
    gram = jnp.concatenate(
        [energy_term, correlation_term, jnp.zeros((VEC, GRAM_PAD - 2 * VEC), jnp.float32)], axis=1
    )
    product, gram = reduce_help(flattened, gram)
    gram = reduce_blk(gram)
    gram = gram / basis_size
    return (product, gram[:, :VEC], gram[:, VEC : 2 * VEC])


def solution(mesh):
    placed = (
        P(None, ("blk", "help")),
        P(("blk", "help"), None, None, None, None),
        P(("blk", "help"), None, None),
        P(("blk", "help"), None, None),
        P(("blk", "help"), None),
    )
    return jax.shard_map(
        local,
        mesh=mesh,
        in_specs=placed,
        out_specs=(P(None, ("blk", "help")), P(), P()),
        check_vma=False,
    )
```

```python
import jax
import jax.numpy as jnp
from jax import lax
from jax.sharding import PartitionSpec as P

VEC = 8
TILE = 256
BAND = 2
SLOTS = 3
NOFF = 5
GRAM_PAD = 128


def shifted(value, axis, steps):
    count = lax.axis_size(axis)
    initial, last = (max(0, -steps), min(count, count - steps))
    return lax.ppermute(value, axis, [(source, source + steps) for source in range(initial, last)])


def is_power_of_two(count):
    return count & (count - 1) == 0


def exchanged(value, axis, mask):
    count = lax.axis_size(axis)
    return lax.ppermute(value, axis, [(source, source ^ mask) for source in range(count)])


def help_order():
    count = lax.axis_size("help")
    if not is_power_of_two(count):
        return jnp.int32(0)
    return lax.axis_index("help").astype(jnp.int32)


def gather_help(piece):
    count = lax.axis_size("help")
    if not is_power_of_two(count):
        return lax.all_gather(piece, "help", axis=1, tiled=True)
    held = piece
    mask = 1
    while mask < count:
        held = jnp.concatenate([held, exchanged(held, "help", mask)], axis=1)
        mask *= 2
    return held


def reduce_help(partial, gram):
    count = lax.axis_size("help")
    if not is_power_of_two(count):
        return (
            lax.psum_scatter(partial, "help", scatter_dimension=1, tiled=True),
            lax.psum(gram, "help"),
        )
    held = partial
    mask = count // 2
    while mask >= 1:
        half = held.shape[1] // 2
        arrived = exchanged(jnp.concatenate([held[:, half:], gram], axis=1), "help", mask)
        held = held[:, :half] + arrived[:, :half]
        gram = gram + arrived[:, half:]
        mask //= 2
    return held, gram


def reduce_blk(gram):
    count = lax.axis_size("blk")
    if not is_power_of_two(count):
        return lax.psum(gram, "blk")
    mask = 1
    while mask < count:
        gram = gram + exchanged(gram, "blk", mask)
        mask *= 2
    return gram


def cyclic(value, axis, steps):
    count = lax.axis_size(axis)
    return lax.ppermute(value, axis, [(source, (source + steps) % count) for source in range(count)])


def neighbour_panels(source):
    width = source.shape[1]
    below = cyclic(source, "blk", 1)
    above = cyclic(jnp.concatenate([below, source], axis=1), "blk", -2)
    further = cyclic(below, "blk", 1)
    return [further, below, source, above[:, :width], above[:, width:]]


def local(vectors, tile_blocks, tile_row, tile_col, counts):
    groups = lax.axis_size("blk")
    piece_width = vectors.shape[1]
    group_width = piece_width * lax.axis_size("help")
    group_rows = group_width // TILE
    full_panel = gather_help(vectors)
    panels = neighbour_panels(full_panel)
    tiles_per_piece = piece_width // TILE
    order = help_order()

    def placed(tile_index):
        return ((tile_index // tiles_per_piece) ^ order) * tiles_per_piece + tile_index % tiles_per_piece

    column_place = placed(tile_col[0])
    row_place = placed(tile_row[0])
    slot_ids = jnp.arange(SLOTS, dtype=jnp.int32)[None, :]
    row_ids = jnp.arange(group_rows, dtype=jnp.int32)
    column_blocks = lax.axis_index("blk") + jnp.arange(NOFF, dtype=jnp.int32) - BAND
    in_band = (column_blocks >= 0) & (column_blocks < groups)
    live = ((slot_ids < counts[0][:, None]) & in_band[:, None]).astype(jnp.float32)
    one_hot = (row_place[:, :, None] == row_ids).astype(jnp.float32) * live[:, :, None]
    partial_value = None
    for batch in ((BAND - 1, BAND), (0, BAND + 1, BAND + 2)):

        def taken(array):
            return jnp.concatenate([array[o : o + 1] for o in batch])

        stacked = jnp.stack([panels[o] for o in batch]).reshape(len(batch), VEC, group_rows, TILE)
        stacked = stacked.transpose(0, 2, 1, 3)
        pieces = stacked[jnp.arange(len(batch))[:, None], taken(column_place)]
        contribution = jnp.einsum(
            "osit,ostu->osiu", pieces, taken(tile_blocks[0]), precision=lax.Precision.HIGH
        )
        batch_value = jnp.einsum(
            "osiu,osr->iru", contribution, taken(one_hot), precision=lax.Precision.HIGHEST
        )
        partial_value = batch_value if partial_value is None else partial_value + batch_value
    flattened = partial_value.reshape(VEC, group_width)
    basis_size = float(groups * group_width)
    correlation_term = jnp.dot(
        vectors, vectors.T, precision=lax.Precision.HIGHEST, preferred_element_type=jnp.float32
    )
    energy_term = jnp.dot(
        full_panel, flattened.T, precision=lax.Precision.HIGHEST, preferred_element_type=jnp.float32
    )
    gram = jnp.concatenate(
        [energy_term, correlation_term, jnp.zeros((VEC, GRAM_PAD - 2 * VEC), jnp.float32)], axis=1
    )
    product, gram = reduce_help(flattened, gram)
    gram = reduce_blk(gram)
    gram = gram / basis_size
    return (product, gram[:, :VEC], gram[:, VEC : 2 * VEC])


def solution(mesh):
    placed = (
        P(None, ("blk", "help")),
        P(("blk", "help"), None, None, None, None),
        P(("blk", "help"), None, None),
        P(("blk", "help"), None, None),
        P(("blk", "help"), None),
    )
    return jax.shard_map(
        local,
        mesh=mesh,
        in_specs=placed,
        out_specs=(P(None, ("blk", "help")), P(), P()),
        check_vma=False,
    )
```

```python
import jax
import jax.numpy as jnp
from jax import lax
from jax.sharding import PartitionSpec as P

VEC = 8
TILE = 256
BAND = 2
SLOTS = 3
NOFF = 5
GRAM_PAD = 128


def shifted(value, axis, steps):
    count = lax.axis_size(axis)
    initial, last = (max(0, -steps), min(count, count - steps))
    return lax.ppermute(value, axis, [(source, source + steps) for source in range(initial, last)])


def is_power_of_two(count):
    return count & (count - 1) == 0


def exchanged(value, axis, mask):
    count = lax.axis_size(axis)
    return lax.ppermute(value, axis, [(source, source ^ mask) for source in range(count)])


def help_order():
    count = lax.axis_size("help")
    if not is_power_of_two(count):
        return jnp.int32(0)
    return lax.axis_index("help").astype(jnp.int32)


def gather_help(piece):
    count = lax.axis_size("help")
    if not is_power_of_two(count):
        return lax.all_gather(piece, "help", axis=1, tiled=True)
    held = piece
    mask = 1
    while mask < count:
        held = jnp.concatenate([held, exchanged(held, "help", mask)], axis=1)
        mask *= 2
    return held


def reduce_help(partial, gram):
    count = lax.axis_size("help")
    if not is_power_of_two(count):
        return (
            lax.psum_scatter(partial, "help", scatter_dimension=1, tiled=True),
            lax.psum(gram, "help"),
        )
    held = partial
    mask = count // 2
    while mask >= 1:
        half = held.shape[1] // 2
        arrived = exchanged(jnp.concatenate([held[:, half:], gram], axis=1), "help", mask)
        held = held[:, :half] + arrived[:, :half]
        gram = gram + arrived[:, half:]
        mask //= 2
    return held, gram


def reduce_blk(gram):
    count = lax.axis_size("blk")
    if not is_power_of_two(count):
        return lax.psum(gram, "blk")
    mask = 1
    while mask < count:
        gram = gram + exchanged(gram, "blk", mask)
        mask *= 2
    return gram


def cyclic(value, axis, steps):
    count = lax.axis_size(axis)
    return lax.ppermute(value, axis, [(source, (source + steps) % count) for source in range(count)])


def neighbour_panels(source):
    width = source.shape[1]
    below = cyclic(source, "blk", 1)
    above = cyclic(jnp.concatenate([below, source], axis=1), "blk", -2)
    further = cyclic(below, "blk", 1)
    return [further, below, source, above[:, :width], above[:, width:]]


def local(vectors, tile_blocks, tile_row, tile_col, counts):
    groups = lax.axis_size("blk")
    piece_width = vectors.shape[1]
    group_width = piece_width * lax.axis_size("help")
    group_rows = group_width // TILE
    full_panel = gather_help(vectors)
    panels = neighbour_panels(full_panel)
    tiles_per_piece = piece_width // TILE
    order = help_order()

    def placed(tile_index):
        return ((tile_index // tiles_per_piece) ^ order) * tiles_per_piece + tile_index % tiles_per_piece

    column_place = placed(tile_col[0])
    row_place = placed(tile_row[0])
    slot_ids = jnp.arange(SLOTS, dtype=jnp.int32)[None, :]
    row_ids = jnp.arange(group_rows, dtype=jnp.int32)
    column_blocks = lax.axis_index("blk") + jnp.arange(NOFF, dtype=jnp.int32) - BAND
    in_band = (column_blocks >= 0) & (column_blocks < groups)
    live = ((slot_ids < counts[0][:, None]) & in_band[:, None]).astype(jnp.float32)
    one_hot = (row_place[:, :, None] == row_ids).astype(jnp.float32) * live[:, :, None]
    partial_value = None
    for batch in ((BAND - 1, BAND), (BAND + 1, BAND + 2), (0,)):

        def taken(array):
            return array[batch[0] : batch[-1] + 1]

        stacked = jnp.stack([panels[o] for o in batch]).reshape(len(batch), VEC, group_rows, TILE)
        stacked = stacked.transpose(0, 2, 1, 3)
        pieces = stacked[jnp.arange(len(batch))[:, None], taken(column_place)]
        contribution = jnp.einsum(
            "osit,ostu->osiu", pieces, taken(tile_blocks[0]), precision=lax.Precision.HIGH
        )
        batch_value = jnp.einsum(
            "osiu,osr->iru", contribution, taken(one_hot), precision=lax.Precision.HIGHEST
        )
        partial_value = batch_value if partial_value is None else partial_value + batch_value
    flattened = partial_value.reshape(VEC, group_width)
    basis_size = float(groups * group_width)
    correlation_term = jnp.dot(
        vectors, vectors.T, precision=lax.Precision.HIGHEST, preferred_element_type=jnp.float32
    )
    energy_term = jnp.dot(
        full_panel, flattened.T, precision=lax.Precision.HIGHEST, preferred_element_type=jnp.float32
    )
    gram = jnp.concatenate(
        [energy_term, correlation_term, jnp.zeros((VEC, GRAM_PAD - 2 * VEC), jnp.float32)], axis=1
    )
    product, gram = reduce_help(flattened, gram)
    gram = reduce_blk(gram)
    gram = gram / basis_size
    return (product, gram[:, :VEC], gram[:, VEC : 2 * VEC])


def solution(mesh):
    placed = (
        P(None, ("blk", "help")),
        P(("blk", "help"), None, None, None, None),
        P(("blk", "help"), None, None),
        P(("blk", "help"), None, None),
        P(("blk", "help"), None),
    )
    return jax.shard_map(
        local,
        mesh=mesh,
        in_specs=placed,
        out_specs=(P(None, ("blk", "help")), P(), P()),
        check_vma=False,
    )
```

```python
import jax
import jax.numpy as jnp
from jax import lax
from jax.experimental import pallas as pl
from jax.experimental.pallas import tpu as pltpu
from jax.sharding import PartitionSpec as P

VEC = 8
TILE = 256
BAND = 2
SLOTS = 3
NOFF = 5
GRAM_PAD = 128


def shifted(value, axis, steps):
    count = lax.axis_size(axis)
    initial, last = (max(0, -steps), min(count, count - steps))
    return lax.ppermute(value, axis, [(source, source + steps) for source in range(initial, last)])


def is_power_of_two(count):
    return count & (count - 1) == 0


def exchanged(value, axis, mask):
    count = lax.axis_size(axis)
    return lax.ppermute(value, axis, [(source, source ^ mask) for source in range(count)])


def help_order():
    count = lax.axis_size("help")
    if not is_power_of_two(count):
        return jnp.int32(0)
    return lax.axis_index("help").astype(jnp.int32)


def gather_help(piece):
    count = lax.axis_size("help")
    if not is_power_of_two(count):
        return lax.all_gather(piece, "help", axis=1, tiled=True)
    held = piece
    mask = 1
    while mask < count:
        held = jnp.concatenate([held, exchanged(held, "help", mask)], axis=1)
        mask *= 2
    return held


def reduce_help(partial, gram):
    count = lax.axis_size("help")
    if not is_power_of_two(count):
        return (
            lax.psum_scatter(partial, "help", scatter_dimension=1, tiled=True),
            lax.psum(gram, "help"),
        )
    held = partial
    mask = count // 2
    while mask >= 1:
        half = held.shape[1] // 2
        arrived = exchanged(jnp.concatenate([held[:, half:], gram], axis=1), "help", mask)
        held = held[:, :half] + arrived[:, :half]
        gram = gram + arrived[:, half:]
        mask //= 2
    return held, gram


def reduce_blk(gram):
    count = lax.axis_size("blk")
    if not is_power_of_two(count):
        return lax.psum(gram, "blk")
    mask = 1
    while mask < count:
        gram = gram + exchanged(gram, "blk", mask)
        mask *= 2
    return gram


def neighbour_panels(source):
    lowers = []
    uppers = []
    current = source
    for hop_index in range(BAND):
        current = shifted(current, "blk", 1)
        lowers.append(current)
    current = source
    for hop_index in range(BAND):
        current = shifted(current, "blk", -1)
        uppers.append(current)
    return lowers[::-1] + [source] + uppers


def tile_products(panel, tile_blocks, offset_index, columns, counts):
    def kernel(columns_ref, counts_ref, piece_ref, tile_ref, out_ref):
        slot = pl.program_id(0)

        @pl.when(slot < counts_ref[offset_index])
        def _():
            out_ref[...] = jnp.dot(
                piece_ref[...],
                tile_ref[...],
                precision=lax.Precision.HIGHEST,
                preferred_element_type=jnp.float32,
            )

        @pl.when(slot >= counts_ref[offset_index])
        def _():
            out_ref[...] = jnp.zeros_like(out_ref)

    def piece_map(slot, columns_ref, counts_ref):
        return (0, columns_ref[offset_index * SLOTS + slot])

    def tile_map(slot, columns_ref, counts_ref):
        kept = jnp.minimum(slot, counts_ref[offset_index] - 1)
        return (0, offset_index, kept, 0, 0)

    return pl.pallas_call(
        kernel,
        grid_spec=pltpu.PrefetchScalarGridSpec(
            num_scalar_prefetch=2,
            grid=(SLOTS,),
            in_specs=[
                pl.BlockSpec((VEC, TILE), piece_map),
                pl.BlockSpec((None, None, None, TILE, TILE), tile_map),
            ],
            out_specs=pl.BlockSpec((None, VEC, TILE), lambda slot, columns_ref, counts_ref: (slot, 0, 0)),
        ),
        out_shape=jax.ShapeDtypeStruct((SLOTS, VEC, TILE), jnp.float32),
    )(columns, counts, panel, tile_blocks)


def local(vectors, tile_blocks, tile_row, tile_col, counts):
    groups = lax.axis_size("blk")
    piece_width = vectors.shape[1]
    group_width = piece_width * lax.axis_size("help")
    group_rows = group_width // TILE
    full_panel = gather_help(vectors)
    panels = neighbour_panels(full_panel)
    tiles_per_piece = piece_width // TILE
    order = help_order()

    def placed(tile_index):
        return ((tile_index // tiles_per_piece) ^ order) * tiles_per_piece + tile_index % tiles_per_piece

    column_place = placed(tile_col[0])
    row_place = placed(tile_row[0])
    slot_ids = jnp.arange(SLOTS, dtype=jnp.int32)[None, :]
    row_ids = jnp.arange(group_rows, dtype=jnp.int32)
    live = (slot_ids < counts[0][:, None]).astype(jnp.float32)
    one_hot = (row_place[:, :, None] == row_ids).astype(jnp.float32) * live[:, :, None]
    columns = column_place.reshape(-1).astype(jnp.int32)
    slot_counts = counts[0].astype(jnp.int32)
    partial_value = None
    for first, last in ((BAND - 1, BAND + 2), (0, NOFF)):
        batch = [o for o in range(first, last) if partial_value is None or o not in (1, 2, 3)]
        contribution = jnp.stack(
            [tile_products(panels[o], tile_blocks, o, columns, slot_counts) for o in batch]
        )
        chosen = jnp.concatenate([one_hot[o : o + 1] for o in batch])
        batch_value = jnp.einsum(
            "osiu,osr->iru", contribution, chosen, precision=lax.Precision.HIGHEST
        )
        partial_value = batch_value if partial_value is None else partial_value + batch_value
    flattened = partial_value.reshape(VEC, group_width)
    basis_size = float(groups * group_width)
    correlation_term = jnp.dot(
        vectors, vectors.T, precision=lax.Precision.HIGHEST, preferred_element_type=jnp.float32
    )
    energy_term = jnp.dot(
        full_panel, flattened.T, precision=lax.Precision.HIGHEST, preferred_element_type=jnp.float32
    )
    gram = jnp.concatenate(
        [energy_term, correlation_term, jnp.zeros((VEC, GRAM_PAD - 2 * VEC), jnp.float32)], axis=1
    )
    product, gram = reduce_help(flattened, gram)
    gram = reduce_blk(gram)
    gram = gram / basis_size
    return (product, gram[:, :VEC], gram[:, VEC : 2 * VEC])


def solution(mesh):
    placed = (
        P(None, ("blk", "help")),
        P(("blk", "help"), None, None, None, None),
        P(("blk", "help"), None, None),
        P(("blk", "help"), None, None),
        P(("blk", "help"), None),
    )
    return jax.shard_map(
        local,
        mesh=mesh,
        in_specs=placed,
        out_specs=(P(None, ("blk", "help")), P(), P()),
        check_vma=False,
    )
```

```python
import jax
import jax.numpy as jnp
from jax import lax
from jax.sharding import PartitionSpec as P

VEC = 8
TILE = 256
BAND = 2
SLOTS = 3
NOFF = 5
GRAM_PAD = 128


def shifted(value, axis, steps):
    count = lax.axis_size(axis)
    initial, last = (max(0, -steps), min(count, count - steps))
    return lax.ppermute(value, axis, [(source, source + steps) for source in range(initial, last)])


def is_power_of_two(count):
    return count & (count - 1) == 0


def exchanged(value, axis, mask):
    count = lax.axis_size(axis)
    return lax.ppermute(value, axis, [(source, source ^ mask) for source in range(count)])


def help_order():
    count = lax.axis_size("help")
    if not is_power_of_two(count):
        return jnp.int32(0)
    return lax.axis_index("help").astype(jnp.int32)


def gather_help(piece):
    count = lax.axis_size("help")
    if not is_power_of_two(count):
        return lax.all_gather(piece, "help", axis=1, tiled=True)
    held = piece
    mask = 1
    while mask < count:
        held = jnp.concatenate([held, exchanged(held, "help", mask)], axis=1)
        mask *= 2
    return held


def reduce_help(partial, gram):
    count = lax.axis_size("help")
    if not is_power_of_two(count):
        return (
            lax.psum_scatter(partial, "help", scatter_dimension=1, tiled=True),
            lax.psum(gram, "help"),
        )
    held = partial
    mask = count // 2
    while mask >= 1:
        half = held.shape[1] // 2
        arrived = exchanged(jnp.concatenate([held[:, half:], gram], axis=1), "help", mask)
        held = held[:, :half] + arrived[:, :half]
        gram = gram + arrived[:, half:]
        mask //= 2
    return held, gram


def reduce_blk(gram):
    count = lax.axis_size("blk")
    if not is_power_of_two(count):
        return lax.psum(gram, "blk")
    mask = 1
    while mask < count:
        gram = gram + exchanged(gram, "blk", mask)
        mask *= 2
    return gram


def neighbour_panels(source):
    lowers = []
    uppers = []
    current = source
    for hop_index in range(BAND):
        current = shifted(current, "blk", 1)
        lowers.append(current)
    current = source
    for hop_index in range(BAND):
        current = shifted(current, "blk", -1)
        uppers.append(current)
    return lowers[::-1] + [source] + uppers


def paired_panels(vectors):
    local_pair = jnp.concatenate([vectors, exchanged(vectors, "blk", 1)], axis=1)
    gathered = gather_help(local_pair)
    lower = shifted(gathered, "blk", 2)
    upper = shifted(gathered, "blk", -2)
    return gathered, [lower, gathered, upper]


def local(vectors, tile_blocks, tile_row, tile_col, counts):
    groups = lax.axis_size("blk")
    piece_width = vectors.shape[1]
    group_width = piece_width * lax.axis_size("help")
    group_rows = group_width // TILE
    paired = groups % 2 == 0 and is_power_of_two(lax.axis_size("help"))
    tiles_per_piece = piece_width // TILE
    order = help_order()

    def placed(tile_index):
        return ((tile_index // tiles_per_piece) ^ order) * tiles_per_piece + tile_index % tiles_per_piece

    slot_ids = jnp.arange(SLOTS, dtype=jnp.int32)[None, :]
    row_ids = jnp.arange(group_rows, dtype=jnp.int32)
    live = (slot_ids < counts[0][:, None]).astype(jnp.float32)
    offset_ids = jnp.arange(NOFF, dtype=jnp.int32)
    if paired:
        gathered, pairs = paired_panels(vectors)
        helpers = lax.axis_size("help")
        halves = [pair.reshape(VEC, helpers, 2, piece_width) for pair in pairs]
        full_panel = halves[1][:, :, 0].reshape(VEC, group_width)
        stacked = jnp.stack([half[:, :, side] for half in halves for side in range(2)])
        stacked = stacked.reshape(2 * len(pairs), VEC, group_rows, TILE)
        core = lax.axis_index("blk") % 2
        panel_ids = offset_ids + 2 * core * (offset_ids % 2)
    else:
        full_panel = gather_help(vectors)
        stacked = jnp.stack(neighbour_panels(full_panel)).reshape(NOFF, VEC, group_rows, TILE)
        panel_ids = offset_ids
    stacked = stacked.transpose(0, 2, 1, 3)
    column_place = placed(tile_col[0])
    row_place = placed(tile_row[0])
    one_hot = (row_place[:, :, None] == row_ids).astype(jnp.float32) * live[:, :, None]
    pieces = stacked[panel_ids[:, None], column_place]
    contribution = jnp.einsum(
        "osit,ostu->osiu", pieces, tile_blocks[0], precision=lax.Precision.HIGH
    )
    partial_value = jnp.einsum(
        "osiu,osr->iru", contribution, one_hot, precision=lax.Precision.HIGHEST
    )
    flattened = partial_value.reshape(VEC, group_width)
    basis_size = float(groups * group_width)
    correlation_term = jnp.dot(
        vectors, vectors.T, precision=lax.Precision.HIGHEST, preferred_element_type=jnp.float32
    )
    energy_term = jnp.dot(
        full_panel, flattened.T, precision=lax.Precision.HIGHEST, preferred_element_type=jnp.float32
    )
    gram = jnp.concatenate(
        [energy_term, correlation_term, jnp.zeros((VEC, GRAM_PAD - 2 * VEC), jnp.float32)], axis=1
    )
    product, gram = reduce_help(flattened, gram)
    gram = reduce_blk(gram)
    gram = gram / basis_size
    return (product, gram[:, :VEC], gram[:, VEC : 2 * VEC])


def solution(mesh):
    placed = (
        P(None, ("blk", "help")),
        P(("blk", "help"), None, None, None, None),
        P(("blk", "help"), None, None),
        P(("blk", "help"), None, None),
        P(("blk", "help"), None),
    )
    return jax.shard_map(
        local,
        mesh=mesh,
        in_specs=placed,
        out_specs=(P(None, ("blk", "help")), P(), P()),
        check_vma=False,
    )
```

```python
import jax
import jax.numpy as jnp
from jax import lax
from jax.sharding import PartitionSpec as P

VEC = 8
TILE = 256
BAND = 2
SLOTS = 3
NOFF = 5
GRAM_PAD = 128


def shifted(value, axis, steps):
    count = lax.axis_size(axis)
    initial, last = (max(0, -steps), min(count, count - steps))
    return lax.ppermute(value, axis, [(source, source + steps) for source in range(initial, last)])


def is_power_of_two(count):
    return count & (count - 1) == 0


def exchanged(value, axis, mask):
    count = lax.axis_size(axis)
    return lax.ppermute(value, axis, [(source, source ^ mask) for source in range(count)])


def help_order():
    count = lax.axis_size("help")
    if not is_power_of_two(count):
        return jnp.int32(0)
    return lax.axis_index("help").astype(jnp.int32)


def gather_help(piece):
    count = lax.axis_size("help")
    if not is_power_of_two(count):
        return lax.all_gather(piece, "help", axis=1, tiled=True)
    held = piece
    mask = 1
    while mask < count:
        held = jnp.concatenate([held, exchanged(held, "help", mask)], axis=1)
        mask *= 2
    return held


def reduce_help(partial, gram):
    count = lax.axis_size("help")
    if not is_power_of_two(count):
        return (
            lax.psum_scatter(partial, "help", scatter_dimension=1, tiled=True),
            lax.psum(gram, "help"),
        )
    held = partial
    mask = count // 2
    while mask >= 1:
        half = held.shape[1] // 2
        arrived = exchanged(jnp.concatenate([held[:, half:], gram], axis=1), "help", mask)
        held = held[:, :half] + arrived[:, :half]
        gram = gram + arrived[:, half:]
        mask //= 2
    return held, gram


def reduce_blk(gram):
    count = lax.axis_size("blk")
    if not is_power_of_two(count):
        return lax.psum(gram, "blk")
    mask = 1
    while mask < count:
        gram = gram + exchanged(gram, "blk", mask)
        mask *= 2
    return gram


def neighbour_panels(source):
    lowers = []
    uppers = []
    current = source
    for hop_index in range(BAND):
        current = shifted(current, "blk", 1)
        lowers.append(current)
    current = source
    for hop_index in range(BAND):
        current = shifted(current, "blk", -1)
        uppers.append(current)
    return lowers[::-1] + [source] + uppers


def paired_panels(vectors):
    local_pair = jnp.concatenate([vectors, exchanged(vectors, "blk", 1)], axis=1)
    gathered = gather_help(local_pair)
    lower = shifted(gathered, "blk", 2)
    upper = shifted(gathered, "blk", -2)
    return gathered, [lower, gathered, upper]


def local(vectors, tile_blocks, tile_row, tile_col, counts):
    groups = lax.axis_size("blk")
    piece_width = vectors.shape[1]
    group_width = piece_width * lax.axis_size("help")
    group_rows = group_width // TILE
    paired = groups % 2 == 0 and is_power_of_two(lax.axis_size("help"))
    tiles_per_piece = piece_width // TILE
    order = help_order()

    def placed(tile_index):
        return ((tile_index // tiles_per_piece) ^ order) * tiles_per_piece + tile_index % tiles_per_piece

    if paired:
        gathered, pairs = paired_panels(vectors)
        tile_row, tile_col, counts, vectors, _ = lax.optimization_barrier(
            (tile_row, tile_col, counts, vectors, gathered)
        )
    slot_ids = jnp.arange(SLOTS, dtype=jnp.int32)[None, :]
    row_ids = jnp.arange(group_rows, dtype=jnp.int32)
    live = (slot_ids < counts[0][:, None]).astype(jnp.float32)
    offset_ids = jnp.arange(NOFF, dtype=jnp.int32)
    if paired:
        helpers = lax.axis_size("help")
        halves = [pair.reshape(VEC, helpers, 2, piece_width) for pair in pairs]
        full_panel = halves[1][:, :, 0].reshape(VEC, group_width)
        stacked = jnp.stack([half[:, :, side] for half in halves for side in range(2)])
        stacked = stacked.reshape(2 * len(pairs), VEC, group_rows, TILE)
        core = lax.axis_index("blk") % 2
        panel_ids = offset_ids + 2 * core * (offset_ids % 2)
    else:
        full_panel = gather_help(vectors)
        stacked = jnp.stack(neighbour_panels(full_panel)).reshape(NOFF, VEC, group_rows, TILE)
        panel_ids = offset_ids
    stacked = stacked.transpose(0, 2, 1, 3)
    column_place = placed(tile_col[0])
    row_place = placed(tile_row[0])
    one_hot = (row_place[:, :, None] == row_ids).astype(jnp.float32) * live[:, :, None]
    pieces = stacked[panel_ids[:, None], column_place]
    contribution = jnp.einsum(
        "osit,ostu->osiu", pieces, tile_blocks[0], precision=lax.Precision.HIGH
    )
    partial_value = jnp.einsum(
        "osiu,osr->iru", contribution, one_hot, precision=lax.Precision.HIGHEST
    )
    flattened = partial_value.reshape(VEC, group_width)
    basis_size = float(groups * group_width)
    correlation_term = jnp.dot(
        vectors, vectors.T, precision=lax.Precision.HIGHEST, preferred_element_type=jnp.float32
    )
    energy_term = jnp.dot(
        full_panel, flattened.T, precision=lax.Precision.HIGHEST, preferred_element_type=jnp.float32
    )
    gram = jnp.concatenate(
        [energy_term, correlation_term, jnp.zeros((VEC, GRAM_PAD - 2 * VEC), jnp.float32)], axis=1
    )
    product, gram = reduce_help(flattened, gram)
    gram = reduce_blk(gram)
    gram = gram / basis_size
    return (product, gram[:, :VEC], gram[:, VEC : 2 * VEC])


def solution(mesh):
    placed = (
        P(None, ("blk", "help")),
        P(("blk", "help"), None, None, None, None),
        P(("blk", "help"), None, None),
        P(("blk", "help"), None, None),
        P(("blk", "help"), None),
    )
    return jax.shard_map(
        local,
        mesh=mesh,
        in_specs=placed,
        out_specs=(P(None, ("blk", "help")), P(), P()),
        check_vma=False,
    )
```

```python
import jax
import jax.numpy as jnp
from jax import lax
from jax.sharding import PartitionSpec as P

VEC = 8
TILE = 256
BAND = 2
SLOTS = 3
NOFF = 5
GRAM_PAD = 128


def shifted(value, axis, steps):
    count = lax.axis_size(axis)
    initial, last = (max(0, -steps), min(count, count - steps))
    return lax.ppermute(value, axis, [(source, source + steps) for source in range(initial, last)])


def is_power_of_two(count):
    return count & (count - 1) == 0


def exchanged(value, axis, mask):
    count = lax.axis_size(axis)
    return lax.ppermute(value, axis, [(source, source ^ mask) for source in range(count)])


def help_order():
    count = lax.axis_size("help")
    if not is_power_of_two(count):
        return jnp.int32(0)
    return lax.axis_index("help").astype(jnp.int32)


def gather_help(piece):
    count = lax.axis_size("help")
    if not is_power_of_two(count):
        return lax.all_gather(piece, "help", axis=1, tiled=True)
    held = piece
    mask = 1
    while mask < count:
        held = jnp.concatenate([held, exchanged(held, "help", mask)], axis=1)
        mask *= 2
    return held


def reduce_help(partial, gram):
    count = lax.axis_size("help")
    if not is_power_of_two(count):
        return (
            lax.psum_scatter(partial, "help", scatter_dimension=1, tiled=True),
            lax.psum(gram, "help"),
        )
    held = partial
    mask = count // 2
    while mask >= 1:
        half = held.shape[1] // 2
        arrived = exchanged(jnp.concatenate([held[:, half:], gram], axis=1), "help", mask)
        held = held[:, :half] + arrived[:, :half]
        gram = gram + arrived[:, half:]
        mask //= 2
    return held, gram


def reduce_blk(gram):
    count = lax.axis_size("blk")
    if not is_power_of_two(count):
        return lax.psum(gram, "blk")
    mask = 1
    while mask < count:
        gram = gram + exchanged(gram, "blk", mask)
        mask *= 2
    return gram


def neighbour_panels(source):
    lowers = []
    uppers = []
    current = source
    for hop_index in range(BAND):
        current = shifted(current, "blk", 1)
        lowers.append(current)
    current = source
    for hop_index in range(BAND):
        current = shifted(current, "blk", -1)
        uppers.append(current)
    return lowers[::-1] + [source] + uppers


def local(vectors, tile_blocks, tile_row, tile_col, counts):
    groups = lax.axis_size("blk")
    piece_width = vectors.shape[1]
    group_width = piece_width * lax.axis_size("help")
    group_rows = group_width // TILE
    paired = groups % 2 == 0 and is_power_of_two(lax.axis_size("help"))
    tiles_per_piece = piece_width // TILE
    order = help_order()

    def placed(tile_index):
        return ((tile_index // tiles_per_piece) ^ order) * tiles_per_piece + tile_index % tiles_per_piece

    core = lax.axis_index("blk") % 2
    if paired:
        full_panel = gather_help(vectors)
        lower = shifted(full_panel, "blk", BAND)
        upper = shifted(full_panel, "blk", -BAND)
        trio = [lower, full_panel, upper]
        partner = exchanged(jnp.concatenate(trio, axis=1), "blk", 1)
        partner = [partner[:, k * group_width : (k + 1) * group_width] for k in range(3)]
        tile_row, tile_col, counts, vectors, _ = lax.optimization_barrier(
            (tile_row, tile_col, counts, vectors, full_panel)
        )
    else:
        full_panel = gather_help(vectors)
        trio = neighbour_panels(full_panel)
    slot_ids = jnp.arange(SLOTS, dtype=jnp.int32)[None, :]
    row_ids = jnp.arange(group_rows, dtype=jnp.int32)
    live = (slot_ids < counts[0][:, None]).astype(jnp.float32)
    column_place = placed(tile_col[0])
    row_place = placed(tile_row[0])
    one_hot = (row_place[:, :, None] == row_ids).astype(jnp.float32) * live[:, :, None]

    def batch_product(sources, panel_ids, first, last, step):
        stacked = jnp.stack(sources).reshape(len(sources), VEC, group_rows, TILE)
        stacked = stacked.transpose(0, 2, 1, 3)
        pieces = stacked[panel_ids[:, None], column_place[first:last:step]]
        contribution = jnp.einsum(
            "osit,ostu->osiu",
            pieces,
            tile_blocks[0, first:last:step],
            precision=lax.Precision.HIGH,
        )
        return jnp.einsum(
            "osiu,osr->iru",
            contribution,
            one_hot[first:last:step],
            precision=lax.Precision.HIGHEST,
        )

    if paired:
        partial_value = batch_product(trio, jnp.arange(3, dtype=jnp.int32), 0, NOFF, BAND)
        partial_value = partial_value + batch_product(
            partner, jnp.arange(2, dtype=jnp.int32) + core, 1, NOFF - 1, BAND
        )
    else:
        partial_value = batch_product(trio, jnp.arange(NOFF, dtype=jnp.int32), 0, NOFF, 1)
    flattened = partial_value.reshape(VEC, group_width)
    basis_size = float(groups * group_width)
    correlation_term = jnp.dot(
        vectors, vectors.T, precision=lax.Precision.HIGHEST, preferred_element_type=jnp.float32
    )
    energy_term = jnp.dot(
        full_panel, flattened.T, precision=lax.Precision.HIGHEST, preferred_element_type=jnp.float32
    )
    gram = jnp.concatenate(
        [energy_term, correlation_term, jnp.zeros((VEC, GRAM_PAD - 2 * VEC), jnp.float32)], axis=1
    )
    product, gram = reduce_help(flattened, gram)
    gram = reduce_blk(gram)
    gram = gram / basis_size
    return (product, gram[:, :VEC], gram[:, VEC : 2 * VEC])


def solution(mesh):
    placed = (
        P(None, ("blk", "help")),
        P(("blk", "help"), None, None, None, None),
        P(("blk", "help"), None, None),
        P(("blk", "help"), None, None),
        P(("blk", "help"), None),
    )
    return jax.shard_map(
        local,
        mesh=mesh,
        in_specs=placed,
        out_specs=(P(None, ("blk", "help")), P(), P()),
        check_vma=False,
    )
```

```python
import jax
import jax.numpy as jnp
from jax import lax
from jax.sharding import PartitionSpec as P

VEC = 8
TILE = 256
BAND = 2
SLOTS = 3
NOFF = 5
GRAM_PAD = 128


def shifted(value, axis, steps):
    count = lax.axis_size(axis)
    initial, last = (max(0, -steps), min(count, count - steps))
    return lax.ppermute(value, axis, [(source, source + steps) for source in range(initial, last)])


def is_power_of_two(count):
    return count & (count - 1) == 0


def exchanged(value, axis, mask):
    count = lax.axis_size(axis)
    return lax.ppermute(value, axis, [(source, source ^ mask) for source in range(count)])


def help_order():
    count = lax.axis_size("help")
    if not is_power_of_two(count):
        return jnp.int32(0)
    return lax.axis_index("help").astype(jnp.int32)


def gather_help(piece):
    count = lax.axis_size("help")
    if not is_power_of_two(count):
        return lax.all_gather(piece, "help", axis=1, tiled=True)
    held = piece
    mask = 1
    while mask < count:
        held = jnp.concatenate([held, exchanged(held, "help", mask)], axis=1)
        mask *= 2
    return held


def reduce_help(partial, gram):
    count = lax.axis_size("help")
    if not is_power_of_two(count):
        return (
            lax.psum_scatter(partial, "help", scatter_dimension=1, tiled=True),
            lax.psum(gram, "help"),
        )
    held = partial
    mask = count // 2
    while mask >= 1:
        half = held.shape[1] // 2
        arrived = exchanged(jnp.concatenate([held[:, half:], gram], axis=1), "help", mask)
        held = held[:, :half] + arrived[:, :half]
        gram = gram + arrived[:, half:]
        mask //= 2
    return held, gram


def reduce_blk(gram):
    count = lax.axis_size("blk")
    if not is_power_of_two(count):
        return lax.psum(gram, "blk")
    mask = 1
    while mask < count:
        gram = gram + exchanged(gram, "blk", mask)
        mask *= 2
    return gram


def neighbour_panels(source):
    lowers = []
    uppers = []
    current = source
    for hop_index in range(BAND):
        current = shifted(current, "blk", 1)
        lowers.append(current)
    current = source
    for hop_index in range(BAND):
        current = shifted(current, "blk", -1)
        uppers.append(current)
    return lowers[::-1] + [source] + uppers


def local(vectors, tile_blocks, tile_row, tile_col, counts):
    groups = lax.axis_size("blk")
    piece_width = vectors.shape[1]
    group_width = piece_width * lax.axis_size("help")
    group_rows = group_width // TILE
    paired = groups % 2 == 0 and is_power_of_two(lax.axis_size("help"))
    tiles_per_piece = piece_width // TILE
    order = help_order()

    def placed(tile_index):
        return ((tile_index // tiles_per_piece) ^ order) * tiles_per_piece + tile_index % tiles_per_piece

    core = lax.axis_index("blk") % 2
    if paired:
        full_panel = gather_help(vectors)
        lower = shifted(full_panel, "blk", BAND)
        upper = shifted(full_panel, "blk", -BAND)
        trio = [lower, full_panel, upper]
        partner = exchanged(jnp.concatenate(trio, axis=1), "blk", 1)
        partner = [partner[:, k * group_width : (k + 1) * group_width] for k in range(3)]
        tile_row, tile_col, counts, vectors, _ = lax.optimization_barrier(
            (tile_row, tile_col, counts, vectors, full_panel)
        )
    else:
        full_panel = gather_help(vectors)
        trio = neighbour_panels(full_panel)
    slot_ids = jnp.arange(SLOTS, dtype=jnp.int32)[None, :]
    row_ids = jnp.arange(group_rows, dtype=jnp.int32)
    live = (slot_ids < counts[0][:, None]).astype(jnp.float32)
    column_place = placed(tile_col[0])
    row_place = placed(tile_row[0])
    one_hot = (row_place[:, :, None] == row_ids).astype(jnp.float32) * live[:, :, None]

    def batch_product(sources, panel_ids, first, last, step):
        stacked = jnp.stack(sources).reshape(len(sources), VEC, group_rows, TILE)
        stacked = stacked.transpose(0, 2, 1, 3)
        pieces = stacked[panel_ids[:, None], column_place[first:last:step]]
        contribution = jnp.einsum(
            "osit,ostu->osiu",
            pieces,
            tile_blocks[0, first:last:step],
            precision=lax.Precision.HIGH,
        )
        return jnp.einsum(
            "osiu,osr->iru",
            contribution,
            one_hot[first:last:step],
            precision=lax.Precision.HIGHEST,
        )

    if paired:
        partial_value = batch_product(trio[1:2], jnp.arange(1, dtype=jnp.int32), BAND, BAND + 1, 1)
        partial_value = partial_value + batch_product(
            [trio[0], trio[2]], jnp.arange(2, dtype=jnp.int32), 0, NOFF, NOFF - 1
        )
        partial_value = partial_value + batch_product(
            partner, jnp.arange(2, dtype=jnp.int32) + core, 1, NOFF - 1, BAND
        )
    else:
        partial_value = batch_product(trio, jnp.arange(NOFF, dtype=jnp.int32), 0, NOFF, 1)
    flattened = partial_value.reshape(VEC, group_width)
    basis_size = float(groups * group_width)
    correlation_term = jnp.dot(
        vectors, vectors.T, precision=lax.Precision.HIGHEST, preferred_element_type=jnp.float32
    )
    energy_term = jnp.dot(
        full_panel, flattened.T, precision=lax.Precision.HIGHEST, preferred_element_type=jnp.float32
    )
    gram = jnp.concatenate(
        [energy_term, correlation_term, jnp.zeros((VEC, GRAM_PAD - 2 * VEC), jnp.float32)], axis=1
    )
    product, gram = reduce_help(flattened, gram)
    gram = reduce_blk(gram)
    gram = gram / basis_size
    return (product, gram[:, :VEC], gram[:, VEC : 2 * VEC])


def solution(mesh):
    placed = (
        P(None, ("blk", "help")),
        P(("blk", "help"), None, None, None, None),
        P(("blk", "help"), None, None),
        P(("blk", "help"), None, None),
        P(("blk", "help"), None),
    )
    return jax.shard_map(
        local,
        mesh=mesh,
        in_specs=placed,
        out_specs=(P(None, ("blk", "help")), P(), P()),
        check_vma=False,
    )
```

```python
import jax
import jax.numpy as jnp
from jax import lax
from jax.sharding import PartitionSpec as P

VEC = 8
TILE = 256
BAND = 2
SLOTS = 3
NOFF = 5
GRAM_PAD = 128


def shifted(value, axis, steps):
    count = lax.axis_size(axis)
    initial, last = (max(0, -steps), min(count, count - steps))
    return lax.ppermute(value, axis, [(source, source + steps) for source in range(initial, last)])


def is_power_of_two(count):
    return count & (count - 1) == 0


def exchanged(value, axis, mask):
    count = lax.axis_size(axis)
    return lax.ppermute(value, axis, [(source, source ^ mask) for source in range(count)])


def help_order():
    count = lax.axis_size("help")
    if not is_power_of_two(count):
        return jnp.int32(0)
    return lax.axis_index("help").astype(jnp.int32)


def gather_help(piece):
    count = lax.axis_size("help")
    if not is_power_of_two(count):
        return lax.all_gather(piece, "help", axis=1, tiled=True)
    held = piece
    mask = 1
    while mask < count:
        held = jnp.concatenate([held, exchanged(held, "help", mask)], axis=1)
        mask *= 2
    return held


def reduce_help(partial, gram):
    count = lax.axis_size("help")
    if not is_power_of_two(count):
        return (
            lax.psum_scatter(partial, "help", scatter_dimension=1, tiled=True),
            lax.psum(gram, "help"),
        )
    held = partial
    mask = count // 2
    while mask >= 1:
        half = held.shape[1] // 2
        arrived = exchanged(jnp.concatenate([held[:, half:], gram], axis=1), "help", mask)
        held = held[:, :half] + arrived[:, :half]
        gram = gram + arrived[:, half:]
        mask //= 2
    return held, gram


def reduce_blk(gram):
    count = lax.axis_size("blk")
    if not is_power_of_two(count):
        return lax.psum(gram, "blk")
    mask = 1
    while mask < count:
        gram = gram + exchanged(gram, "blk", mask)
        mask *= 2
    return gram


def neighbour_panels(source):
    lowers = []
    uppers = []
    current = source
    for hop_index in range(BAND):
        current = shifted(current, "blk", 1)
        lowers.append(current)
    current = source
    for hop_index in range(BAND):
        current = shifted(current, "blk", -1)
        uppers.append(current)
    return lowers[::-1] + [source] + uppers


def local(vectors, tile_blocks, tile_row, tile_col, counts):
    groups = lax.axis_size("blk")
    piece_width = vectors.shape[1]
    group_width = piece_width * lax.axis_size("help")
    group_rows = group_width // TILE
    paired = groups % 2 == 0 and is_power_of_two(lax.axis_size("help"))
    tiles_per_piece = piece_width // TILE
    order = help_order()

    def placed(tile_index):
        return ((tile_index // tiles_per_piece) ^ order) * tiles_per_piece + tile_index % tiles_per_piece

    core = lax.axis_index("blk") % 2
    if paired:
        full_panel = gather_help(vectors)
        lower = shifted(full_panel, "blk", BAND)
        upper = shifted(full_panel, "blk", -BAND)
        trio = [lower, full_panel, upper]
        partner = exchanged(jnp.concatenate(trio, axis=1), "blk", 1)
        partner = [partner[:, k * group_width : (k + 1) * group_width] for k in range(3)]
        tile_row, tile_col, counts, vectors, _ = lax.optimization_barrier(
            (tile_row, tile_col, counts, vectors, full_panel)
        )
    else:
        full_panel = gather_help(vectors)
        trio = neighbour_panels(full_panel)
    slot_ids = jnp.arange(SLOTS, dtype=jnp.int32)[None, :]
    row_ids = jnp.arange(group_rows, dtype=jnp.int32)
    live = (slot_ids < counts[0][:, None]).astype(jnp.float32)
    column_place = placed(tile_col[0])
    row_place = placed(tile_row[0])
    one_hot = (row_place[:, :, None] == row_ids).astype(jnp.float32) * live[:, :, None]

    def batch_product(sources, panel_ids, first, last, step):
        stacked = jnp.stack(sources).reshape(len(sources), VEC, group_rows, TILE)
        stacked = stacked.transpose(0, 2, 1, 3)
        pieces = stacked[panel_ids[:, None], column_place[first:last:step]]
        contribution = jnp.einsum(
            "osit,ostu->osiu",
            pieces,
            tile_blocks[0, first:last:step],
            precision=lax.Precision.HIGH,
        )
        return jnp.einsum(
            "osiu,osr->iru",
            contribution,
            one_hot[first:last:step],
            precision=lax.Precision.HIGHEST,
        )

    if paired:
        partial_value = batch_product(
            [trio[0], trio[2]], jnp.arange(2, dtype=jnp.int32), 0, NOFF, NOFF - 1
        )
        middle_ids = jnp.stack([core, jnp.int32(3), core + 1]).astype(jnp.int32)
        partial_value = partial_value + batch_product(
            partner + [trio[1]], middle_ids, BAND - 1, BAND + 2, 1
        )
    else:
        partial_value = batch_product(trio, jnp.arange(NOFF, dtype=jnp.int32), 0, NOFF, 1)
    flattened = partial_value.reshape(VEC, group_width)
    basis_size = float(groups * group_width)
    correlation_term = jnp.dot(
        vectors, vectors.T, precision=lax.Precision.HIGHEST, preferred_element_type=jnp.float32
    )
    energy_term = jnp.dot(
        full_panel, flattened.T, precision=lax.Precision.HIGHEST, preferred_element_type=jnp.float32
    )
    gram = jnp.concatenate(
        [energy_term, correlation_term, jnp.zeros((VEC, GRAM_PAD - 2 * VEC), jnp.float32)], axis=1
    )
    product, gram = reduce_help(flattened, gram)
    gram = reduce_blk(gram)
    gram = gram / basis_size
    return (product, gram[:, :VEC], gram[:, VEC : 2 * VEC])


def solution(mesh):
    placed = (
        P(None, ("blk", "help")),
        P(("blk", "help"), None, None, None, None),
        P(("blk", "help"), None, None),
        P(("blk", "help"), None, None),
        P(("blk", "help"), None),
    )
    return jax.shard_map(
        local,
        mesh=mesh,
        in_specs=placed,
        out_specs=(P(None, ("blk", "help")), P(), P()),
        check_vma=False,
    )
```

```python
import jax
import jax.numpy as jnp
from jax import lax
from jax.sharding import PartitionSpec as P

VEC = 8
TILE = 256
BAND = 2
SLOTS = 3
NOFF = 5
GRAM_PAD = 128


def shifted(value, axis, steps):
    count = lax.axis_size(axis)
    initial, last = (max(0, -steps), min(count, count - steps))
    return lax.ppermute(value, axis, [(source, source + steps) for source in range(initial, last)])


def is_power_of_two(count):
    return count & (count - 1) == 0


def exchanged(value, axis, mask):
    count = lax.axis_size(axis)
    return lax.ppermute(value, axis, [(source, source ^ mask) for source in range(count)])


def help_order():
    count = lax.axis_size("help")
    if not is_power_of_two(count):
        return jnp.int32(0)
    return lax.axis_index("help").astype(jnp.int32)


def gather_help(piece):
    count = lax.axis_size("help")
    if not is_power_of_two(count):
        return lax.all_gather(piece, "help", axis=1, tiled=True)
    held = piece
    mask = 1
    while mask < count:
        held = jnp.concatenate([held, exchanged(held, "help", mask)], axis=1)
        mask *= 2
    return held


def reduce_help(partial, gram):
    count = lax.axis_size("help")
    if not is_power_of_two(count):
        return (
            lax.psum_scatter(partial, "help", scatter_dimension=1, tiled=True),
            lax.psum(gram, "help"),
        )
    held = partial
    mask = count // 2
    while mask >= 1:
        half = held.shape[1] // 2
        arrived = exchanged(jnp.concatenate([held[:, half:], gram], axis=1), "help", mask)
        held = held[:, :half] + arrived[:, :half]
        gram = gram + arrived[:, half:]
        mask //= 2
    return held, gram


def reduce_blk(gram):
    count = lax.axis_size("blk")
    if not is_power_of_two(count):
        return lax.psum(gram, "blk")
    mask = 1
    while mask < count:
        gram = gram + exchanged(gram, "blk", mask)
        mask *= 2
    return gram


def neighbour_panels(source):
    lowers = []
    uppers = []
    current = source
    for hop_index in range(BAND):
        current = shifted(current, "blk", 1)
        lowers.append(current)
    current = source
    for hop_index in range(BAND):
        current = shifted(current, "blk", -1)
        uppers.append(current)
    return lowers[::-1] + [source] + uppers


def local(vectors, tile_blocks, tile_row, tile_col, counts):
    groups = lax.axis_size("blk")
    piece_width = vectors.shape[1]
    group_width = piece_width * lax.axis_size("help")
    group_rows = group_width // TILE
    paired = groups % 2 == 0 and is_power_of_two(lax.axis_size("help"))
    tiles_per_piece = piece_width // TILE
    order = help_order()

    def placed(tile_index):
        return ((tile_index // tiles_per_piece) ^ order) * tiles_per_piece + tile_index % tiles_per_piece

    core = lax.axis_index("blk") % 2
    if paired:
        helpers = lax.axis_size("help")
        own_pair = gather_help(jnp.concatenate([vectors, exchanged(vectors, "blk", 1)], axis=1))
        crossing = [(b, b + 2) for b in range(0, groups - 2, 2)]
        crossing += [(b, b - 2) for b in range(3, groups, 2)]
        remote = lax.ppermute(own_pair, "blk", crossing)
        partner_remote = exchanged(remote, "blk", 1)
        sources = []
        for pair in (own_pair, remote, partner_remote):
            halves = pair.reshape(VEC, helpers, 2, piece_width)
            sources += [halves[:, :, side].reshape(VEC, group_width) for side in range(2)]
        full_panel = sources[0]
        tile_row, tile_col, counts, vectors, _ = lax.optimization_barrier(
            (tile_row, tile_col, counts, vectors, own_pair)
        )
    else:
        full_panel = gather_help(vectors)
        sources = neighbour_panels(full_panel)
    slot_ids = jnp.arange(SLOTS, dtype=jnp.int32)[None, :]
    row_ids = jnp.arange(group_rows, dtype=jnp.int32)
    live = (slot_ids < counts[0][:, None]).astype(jnp.float32)
    column_place = placed(tile_col[0])
    row_place = placed(tile_row[0])
    one_hot = (row_place[:, :, None] == row_ids).astype(jnp.float32) * live[:, :, None]

    def batch_product(sources, panel_ids, first, last, step):
        stacked = jnp.stack(sources).reshape(len(sources), VEC, group_rows, TILE)
        stacked = stacked.transpose(0, 2, 1, 3)
        pieces = stacked[panel_ids[:, None], column_place[first:last:step]]
        contribution = jnp.einsum(
            "osit,ostu->osiu",
            pieces,
            tile_blocks[0, first:last:step],
            precision=lax.Precision.HIGH,
        )
        return jnp.einsum(
            "osiu,osr->iru",
            contribution,
            one_hot[first:last:step],
            precision=lax.Precision.HIGHEST,
        )

    if paired:
        panel_ids = jnp.where(
            core == 0,
            jnp.array([2, 3, 0, 1, 5], dtype=jnp.int32),
            jnp.array([5, 1, 0, 3, 2], dtype=jnp.int32),
        )
    else:
        panel_ids = jnp.arange(NOFF, dtype=jnp.int32)
    partial_value = batch_product(sources, panel_ids, 0, NOFF, 1)
    flattened = partial_value.reshape(VEC, group_width)
    basis_size = float(groups * group_width)
    correlation_term = jnp.dot(
        vectors, vectors.T, precision=lax.Precision.HIGHEST, preferred_element_type=jnp.float32
    )
    energy_term = jnp.dot(
        full_panel, flattened.T, precision=lax.Precision.HIGHEST, preferred_element_type=jnp.float32
    )
    gram = jnp.concatenate(
        [energy_term, correlation_term, jnp.zeros((VEC, GRAM_PAD - 2 * VEC), jnp.float32)], axis=1
    )
    product, gram = reduce_help(flattened, gram)
    gram = reduce_blk(gram)
    gram = gram / basis_size
    return (product, gram[:, :VEC], gram[:, VEC : 2 * VEC])


def solution(mesh):
    placed = (
        P(None, ("blk", "help")),
        P(("blk", "help"), None, None, None, None),
        P(("blk", "help"), None, None),
        P(("blk", "help"), None, None),
        P(("blk", "help"), None),
    )
    return jax.shard_map(
        local,
        mesh=mesh,
        in_specs=placed,
        out_specs=(P(None, ("blk", "help")), P(), P()),
        check_vma=False,
    )
```

```python
import jax
import jax.numpy as jnp
from jax import lax
from jax.sharding import PartitionSpec as P

VEC = 8
TILE = 256
BAND = 2
SLOTS = 3
NOFF = 5
GRAM_PAD = 128


def shifted(value, axis, steps):
    count = lax.axis_size(axis)
    initial, last = (max(0, -steps), min(count, count - steps))
    return lax.ppermute(value, axis, [(source, source + steps) for source in range(initial, last)])


def is_power_of_two(count):
    return count & (count - 1) == 0


def exchanged(value, axis, mask):
    count = lax.axis_size(axis)
    return lax.ppermute(value, axis, [(source, source ^ mask) for source in range(count)])


def help_order():
    count = lax.axis_size("help")
    if not is_power_of_two(count):
        return jnp.int32(0)
    return lax.axis_index("help").astype(jnp.int32)


def gather_help(piece):
    count = lax.axis_size("help")
    if not is_power_of_two(count):
        return lax.all_gather(piece, "help", axis=1, tiled=True)
    held = piece
    mask = 1
    while mask < count:
        held = jnp.concatenate([held, exchanged(held, "help", mask)], axis=1)
        mask *= 2
    return held


def reduce_help(partial, gram):
    count = lax.axis_size("help")
    if not is_power_of_two(count):
        return (
            lax.psum_scatter(partial, "help", scatter_dimension=1, tiled=True),
            lax.psum(gram, "help"),
        )
    held = partial
    mask = count // 2
    while mask >= 1:
        half = held.shape[1] // 2
        arrived = exchanged(jnp.concatenate([held[:, half:], gram], axis=1), "help", mask)
        held = held[:, :half] + arrived[:, :half]
        gram = gram + arrived[:, half:]
        mask //= 2
    return held, gram


def reduce_blk(gram):
    count = lax.axis_size("blk")
    if not is_power_of_two(count):
        return lax.psum(gram, "blk")
    mask = 1
    while mask < count:
        gram = gram + exchanged(gram, "blk", mask)
        mask *= 2
    return gram


def neighbour_panels(source):
    lowers = []
    uppers = []
    current = source
    for hop_index in range(BAND):
        current = shifted(current, "blk", 1)
        lowers.append(current)
    current = source
    for hop_index in range(BAND):
        current = shifted(current, "blk", -1)
        uppers.append(current)
    return lowers[::-1] + [source] + uppers


def local(vectors, tile_blocks, tile_row, tile_col, counts):
    groups = lax.axis_size("blk")
    piece_width = vectors.shape[1]
    group_width = piece_width * lax.axis_size("help")
    group_rows = group_width // TILE
    paired = groups % 2 == 0 and is_power_of_two(lax.axis_size("help"))
    tiles_per_piece = piece_width // TILE
    order = help_order()

    def placed(tile_index):
        return ((tile_index // tiles_per_piece) ^ order) * tiles_per_piece + tile_index % tiles_per_piece

    core = lax.axis_index("blk") % 2
    if paired:
        helpers = lax.axis_size("help")
        own_pair = jnp.concatenate([vectors, exchanged(vectors, "blk", 1)], axis=1)
        own_pair = jnp.concatenate([own_pair, exchanged(own_pair, "help", 1)], axis=1)
        tile_row, tile_col, counts, vectors, _ = lax.optimization_barrier(
            (tile_row, tile_col, counts, vectors, own_pair)
        )
        mask = 2
        while mask < helpers:
            own_pair = jnp.concatenate([own_pair, exchanged(own_pair, "help", mask)], axis=1)
            mask *= 2
        crossing = [(b, b + 2) for b in range(0, groups - 2, 2)]
        crossing += [(b, b - 2) for b in range(3, groups, 2)]
        remote = lax.ppermute(own_pair, "blk", crossing)
        partner_remote = exchanged(remote, "blk", 1)
        sources = []
        for pair in (own_pair, remote, partner_remote):
            halves = pair.reshape(VEC, helpers, 2, piece_width)
            sources += [halves[:, :, side].reshape(VEC, group_width) for side in range(2)]
        full_panel = sources[0]
    else:
        full_panel = gather_help(vectors)
        sources = neighbour_panels(full_panel)
    slot_ids = jnp.arange(SLOTS, dtype=jnp.int32)[None, :]
    row_ids = jnp.arange(group_rows, dtype=jnp.int32)
    live = (slot_ids < counts[0][:, None]).astype(jnp.float32)
    column_place = placed(tile_col[0])
    row_place = placed(tile_row[0])
    one_hot = (row_place[:, :, None] == row_ids).astype(jnp.float32) * live[:, :, None]

    def batch_product(sources, panel_ids, first, last, step):
        stacked = jnp.stack(sources).reshape(len(sources), VEC, group_rows, TILE)
        stacked = stacked.transpose(0, 2, 1, 3)
        pieces = stacked[panel_ids[:, None], column_place[first:last:step]]
        contribution = jnp.einsum(
            "osit,ostu->osiu",
            pieces,
            tile_blocks[0, first:last:step],
            precision=lax.Precision.HIGH,
        )
        return jnp.einsum(
            "osiu,osr->iru",
            contribution,
            one_hot[first:last:step],
            precision=lax.Precision.HIGHEST,
        )

    if paired:
        panel_ids = jnp.where(
            core == 0,
            jnp.array([2, 3, 0, 1, 5], dtype=jnp.int32),
            jnp.array([5, 1, 0, 3, 2], dtype=jnp.int32),
        )
    else:
        panel_ids = jnp.arange(NOFF, dtype=jnp.int32)
    partial_value = batch_product(sources, panel_ids, 0, NOFF, 1)
    flattened = partial_value.reshape(VEC, group_width)
    basis_size = float(groups * group_width)
    correlation_term = jnp.dot(
        vectors, vectors.T, precision=lax.Precision.HIGHEST, preferred_element_type=jnp.float32
    )
    energy_term = jnp.dot(
        full_panel, flattened.T, precision=lax.Precision.HIGHEST, preferred_element_type=jnp.float32
    )
    gram = jnp.concatenate(
        [energy_term, correlation_term, jnp.zeros((VEC, GRAM_PAD - 2 * VEC), jnp.float32)], axis=1
    )
    product, gram = reduce_help(flattened, gram)
    gram = reduce_blk(gram)
    gram = gram / basis_size
    return (product, gram[:, :VEC], gram[:, VEC : 2 * VEC])


def solution(mesh):
    placed = (
        P(None, ("blk", "help")),
        P(("blk", "help"), None, None, None, None),
        P(("blk", "help"), None, None),
        P(("blk", "help"), None, None),
        P(("blk", "help"), None),
    )
    return jax.shard_map(
        local,
        mesh=mesh,
        in_specs=placed,
        out_specs=(P(None, ("blk", "help")), P(), P()),
        check_vma=False,
    )
```

```python
import jax
import jax.numpy as jnp
from jax import lax
from jax.sharding import PartitionSpec as P

VEC = 8
TILE = 256
BAND = 2
SLOTS = 3
NOFF = 5
GRAM_PAD = 128


def shifted(value, axis, steps):
    count = lax.axis_size(axis)
    initial, last = (max(0, -steps), min(count, count - steps))
    return lax.ppermute(value, axis, [(source, source + steps) for source in range(initial, last)])


def is_power_of_two(count):
    return count & (count - 1) == 0


def exchanged(value, axis, mask):
    count = lax.axis_size(axis)
    return lax.ppermute(value, axis, [(source, source ^ mask) for source in range(count)])


def help_order():
    count = lax.axis_size("help")
    if not is_power_of_two(count):
        return jnp.int32(0)
    return lax.axis_index("help").astype(jnp.int32)


def gather_help(piece):
    count = lax.axis_size("help")
    if not is_power_of_two(count):
        return lax.all_gather(piece, "help", axis=1, tiled=True)
    held = piece
    mask = 1
    while mask < count:
        held = jnp.concatenate([held, exchanged(held, "help", mask)], axis=1)
        mask *= 2
    return held


def reduce_help(partial, gram):
    count = lax.axis_size("help")
    if not is_power_of_two(count):
        return (
            lax.psum_scatter(partial, "help", scatter_dimension=1, tiled=True),
            lax.psum(gram, "help"),
        )
    held = partial
    mask = count // 2
    while mask >= 1:
        half = held.shape[1] // 2
        arrived = exchanged(jnp.concatenate([held[:, half:], gram], axis=1), "help", mask)
        held = held[:, :half] + arrived[:, :half]
        gram = gram + arrived[:, half:]
        mask //= 2
    return held, gram


def reduce_blk(gram):
    count = lax.axis_size("blk")
    if not is_power_of_two(count):
        return lax.psum(gram, "blk")
    mask = 1
    while mask < count:
        gram = gram + exchanged(gram, "blk", mask)
        mask *= 2
    return gram


def neighbour_panels(source):
    lowers = []
    uppers = []
    current = source
    for hop_index in range(BAND):
        current = shifted(current, "blk", 1)
        lowers.append(current)
    current = source
    for hop_index in range(BAND):
        current = shifted(current, "blk", -1)
        uppers.append(current)
    return lowers[::-1] + [source] + uppers


def local(vectors, tile_blocks, tile_row, tile_col, counts):
    groups = lax.axis_size("blk")
    piece_width = vectors.shape[1]
    group_width = piece_width * lax.axis_size("help")
    group_rows = group_width // TILE
    paired = groups % 2 == 0 and is_power_of_two(lax.axis_size("help"))
    tiles_per_piece = piece_width // TILE
    order = help_order()

    def placed(tile_index):
        return ((tile_index // tiles_per_piece) ^ order) * tiles_per_piece + tile_index % tiles_per_piece

    core = lax.axis_index("blk") % 2
    if paired:
        helpers = lax.axis_size("help")
        own_pair = jnp.concatenate([vectors, exchanged(vectors, "blk", 1)], axis=1)
        vectors, _ = lax.optimization_barrier((vectors, own_pair))
        own_pair = jnp.concatenate([own_pair, exchanged(own_pair, "help", 1)], axis=1)
        tile_row, tile_col, counts, _ = lax.optimization_barrier(
            (tile_row, tile_col, counts, own_pair)
        )
        mask = 2
        while mask < helpers:
            own_pair = jnp.concatenate([own_pair, exchanged(own_pair, "help", mask)], axis=1)
            mask *= 2
        crossing = [(b, b + 2) for b in range(0, groups - 2, 2)]
        crossing += [(b, b - 2) for b in range(3, groups, 2)]
        remote = lax.ppermute(own_pair, "blk", crossing)
        partner_remote = exchanged(remote, "blk", 1)
        sources = []
        for pair in (own_pair, remote, partner_remote):
            halves = pair.reshape(VEC, helpers, 2, piece_width)
            sources += [halves[:, :, side].reshape(VEC, group_width) for side in range(2)]
        full_panel = sources[0]
    else:
        full_panel = gather_help(vectors)
        sources = neighbour_panels(full_panel)
    slot_ids = jnp.arange(SLOTS, dtype=jnp.int32)[None, :]
    row_ids = jnp.arange(group_rows, dtype=jnp.int32)
    live = (slot_ids < counts[0][:, None]).astype(jnp.float32)
    column_place = placed(tile_col[0])
    row_place = placed(tile_row[0])
    one_hot = (row_place[:, :, None] == row_ids).astype(jnp.float32) * live[:, :, None]

    def batch_product(sources, panel_ids, first, last, step):
        stacked = jnp.stack(sources).reshape(len(sources), VEC, group_rows, TILE)
        stacked = stacked.transpose(0, 2, 1, 3)
        pieces = stacked[panel_ids[:, None], column_place[first:last:step]]
        contribution = jnp.einsum(
            "osit,ostu->osiu",
            pieces,
            tile_blocks[0, first:last:step],
            precision=lax.Precision.HIGH,
        )
        return jnp.einsum(
            "osiu,osr->iru",
            contribution,
            one_hot[first:last:step],
            precision=lax.Precision.HIGHEST,
        )

    if paired:
        panel_ids = jnp.where(
            core == 0,
            jnp.array([2, 3, 0, 1, 5], dtype=jnp.int32),
            jnp.array([5, 1, 0, 3, 2], dtype=jnp.int32),
        )
    else:
        panel_ids = jnp.arange(NOFF, dtype=jnp.int32)
    partial_value = batch_product(sources, panel_ids, 0, NOFF, 1)
    flattened = partial_value.reshape(VEC, group_width)
    basis_size = float(groups * group_width)
    correlation_term = jnp.dot(
        vectors, vectors.T, precision=lax.Precision.HIGHEST, preferred_element_type=jnp.float32
    )
    energy_term = jnp.dot(
        full_panel, flattened.T, precision=lax.Precision.HIGHEST, preferred_element_type=jnp.float32
    )
    gram = jnp.concatenate(
        [energy_term, correlation_term, jnp.zeros((VEC, GRAM_PAD - 2 * VEC), jnp.float32)], axis=1
    )
    product, gram = reduce_help(flattened, gram)
    gram = reduce_blk(gram)
    gram = gram / basis_size
    return (product, gram[:, :VEC], gram[:, VEC : 2 * VEC])


def solution(mesh):
    placed = (
        P(None, ("blk", "help")),
        P(("blk", "help"), None, None, None, None),
        P(("blk", "help"), None, None),
        P(("blk", "help"), None, None),
        P(("blk", "help"), None),
    )
    return jax.shard_map(
        local,
        mesh=mesh,
        in_specs=placed,
        out_specs=(P(None, ("blk", "help")), P(), P()),
        check_vma=False,
    )
```

```python
import jax
import jax.numpy as jnp
from jax import lax
from jax.sharding import PartitionSpec as P

VEC = 8
TILE = 256
BAND = 2
SLOTS = 3
NOFF = 5
GRAM_PAD = 128


def shifted(value, axis, steps):
    count = lax.axis_size(axis)
    initial, last = (max(0, -steps), min(count, count - steps))
    return lax.ppermute(value, axis, [(source, source + steps) for source in range(initial, last)])


def is_power_of_two(count):
    return count & (count - 1) == 0


def exchanged(value, axis, mask):
    count = lax.axis_size(axis)
    return lax.ppermute(value, axis, [(source, source ^ mask) for source in range(count)])


def help_order():
    count = lax.axis_size("help")
    if not is_power_of_two(count):
        return jnp.int32(0)
    return lax.axis_index("help").astype(jnp.int32)


def gather_help(piece):
    count = lax.axis_size("help")
    if not is_power_of_two(count):
        return lax.all_gather(piece, "help", axis=1, tiled=True)
    held = piece
    mask = 1
    while mask < count:
        held = jnp.concatenate([held, exchanged(held, "help", mask)], axis=1)
        mask *= 2
    return held


def reduce_help(partial, gram):
    count = lax.axis_size("help")
    if not is_power_of_two(count):
        return (
            lax.psum_scatter(partial, "help", scatter_dimension=1, tiled=True),
            lax.psum(gram, "help"),
        )
    held = partial
    mask = count // 2
    while mask >= 1:
        half = held.shape[1] // 2
        arrived = exchanged(jnp.concatenate([held[:, half:], gram], axis=1), "help", mask)
        held = held[:, :half] + arrived[:, :half]
        gram = gram + arrived[:, half:]
        mask //= 2
    return held, gram


def reduce_blk(gram):
    count = lax.axis_size("blk")
    if not is_power_of_two(count):
        return lax.psum(gram, "blk")
    mask = 1
    while mask < count:
        gram = gram + exchanged(gram, "blk", mask)
        mask *= 2
    return gram


def neighbour_panels(source):
    lowers = []
    uppers = []
    current = source
    for hop_index in range(BAND):
        current = shifted(current, "blk", 1)
        lowers.append(current)
    current = source
    for hop_index in range(BAND):
        current = shifted(current, "blk", -1)
        uppers.append(current)
    return lowers[::-1] + [source] + uppers


def local(vectors, tile_blocks, tile_row, tile_col, counts):
    groups = lax.axis_size("blk")
    piece_width = vectors.shape[1]
    group_width = piece_width * lax.axis_size("help")
    group_rows = group_width // TILE
    paired = groups % 2 == 0 and is_power_of_two(lax.axis_size("help"))
    tiles_per_piece = piece_width // TILE
    order = help_order()

    def placed(tile_index):
        return ((tile_index // tiles_per_piece) ^ order) * tiles_per_piece + tile_index % tiles_per_piece

    core = lax.axis_index("blk") % 2
    if paired:
        helpers = lax.axis_size("help")
        own_pair = jnp.concatenate([vectors, exchanged(vectors, "blk", 1)], axis=1)
        vectors, _ = lax.optimization_barrier((vectors, own_pair))
        own_pair = jnp.concatenate([own_pair, exchanged(own_pair, "help", 1)], axis=1)
        tile_col, _ = lax.optimization_barrier((tile_col, own_pair))
        mask = 2
        while mask < helpers:
            own_pair = jnp.concatenate([own_pair, exchanged(own_pair, "help", mask)], axis=1)
            mask *= 2
        tile_row, counts, _ = lax.optimization_barrier((tile_row, counts, own_pair))
        crossing = [(b, b + 2) for b in range(0, groups - 2, 2)]
        crossing += [(b, b - 2) for b in range(3, groups, 2)]
        remote = lax.ppermute(own_pair, "blk", crossing)
        partner_remote = exchanged(remote, "blk", 1)
        sources = []
        for pair in (own_pair, remote, partner_remote):
            halves = pair.reshape(VEC, helpers, 2, piece_width)
            sources += [halves[:, :, side].reshape(VEC, group_width) for side in range(2)]
        full_panel = sources[0]
    else:
        full_panel = gather_help(vectors)
        sources = neighbour_panels(full_panel)
    slot_ids = jnp.arange(SLOTS, dtype=jnp.int32)[None, :]
    row_ids = jnp.arange(group_rows, dtype=jnp.int32)
    live = (slot_ids < counts[0][:, None]).astype(jnp.float32)
    column_place = placed(tile_col[0])
    row_place = placed(tile_row[0])
    one_hot = (row_place[:, :, None] == row_ids).astype(jnp.float32) * live[:, :, None]

    def batch_product(sources, panel_ids, first, last, step):
        stacked = jnp.stack(sources).reshape(len(sources), VEC, group_rows, TILE)
        stacked = stacked.transpose(0, 2, 1, 3)
        pieces = stacked[panel_ids[:, None], column_place[first:last:step]]
        contribution = jnp.einsum(
            "osit,ostu->osiu",
            pieces,
            tile_blocks[0, first:last:step],
            precision=lax.Precision.HIGH,
        )
        return jnp.einsum(
            "osiu,osr->iru",
            contribution,
            one_hot[first:last:step],
            precision=lax.Precision.HIGHEST,
        )

    if paired:
        panel_ids = jnp.where(
            core == 0,
            jnp.array([2, 3, 0, 1, 5], dtype=jnp.int32),
            jnp.array([5, 1, 0, 3, 2], dtype=jnp.int32),
        )
    else:
        panel_ids = jnp.arange(NOFF, dtype=jnp.int32)
    partial_value = batch_product(sources, panel_ids, 0, NOFF, 1)
    flattened = partial_value.reshape(VEC, group_width)
    basis_size = float(groups * group_width)
    correlation_term = jnp.dot(
        vectors, vectors.T, precision=lax.Precision.HIGHEST, preferred_element_type=jnp.float32
    )
    energy_term = jnp.dot(
        full_panel, flattened.T, precision=lax.Precision.HIGHEST, preferred_element_type=jnp.float32
    )
    gram = jnp.concatenate(
        [energy_term, correlation_term, jnp.zeros((VEC, GRAM_PAD - 2 * VEC), jnp.float32)], axis=1
    )
    product, gram = reduce_help(flattened, gram)
    gram = reduce_blk(gram)
    gram = gram / basis_size
    return (product, gram[:, :VEC], gram[:, VEC : 2 * VEC])


def solution(mesh):
    placed = (
        P(None, ("blk", "help")),
        P(("blk", "help"), None, None, None, None),
        P(("blk", "help"), None, None),
        P(("blk", "help"), None, None),
        P(("blk", "help"), None),
    )
    return jax.shard_map(
        local,
        mesh=mesh,
        in_specs=placed,
        out_specs=(P(None, ("blk", "help")), P(), P()),
        check_vma=False,
    )
```

```python
import jax
import jax.numpy as jnp
from jax import lax
from jax.sharding import PartitionSpec as P

VEC = 8
TILE = 256
BAND = 2
SLOTS = 3
NOFF = 5
GRAM_PAD = 128


def shifted(value, axis, steps):
    count = lax.axis_size(axis)
    initial, last = (max(0, -steps), min(count, count - steps))
    return lax.ppermute(value, axis, [(source, source + steps) for source in range(initial, last)])


def is_power_of_two(count):
    return count & (count - 1) == 0


def exchanged(value, axis, mask):
    count = lax.axis_size(axis)
    return lax.ppermute(value, axis, [(source, source ^ mask) for source in range(count)])


def help_order():
    count = lax.axis_size("help")
    if not is_power_of_two(count):
        return jnp.int32(0)
    return lax.axis_index("help").astype(jnp.int32)


def gather_help(piece):
    count = lax.axis_size("help")
    if not is_power_of_two(count):
        return lax.all_gather(piece, "help", axis=1, tiled=True)
    held = piece
    mask = 1
    while mask < count:
        held = jnp.concatenate([held, exchanged(held, "help", mask)], axis=1)
        mask *= 2
    return held


def reduce_help(partial, gram):
    count = lax.axis_size("help")
    if not is_power_of_two(count):
        return (
            lax.psum_scatter(partial, "help", scatter_dimension=1, tiled=True),
            lax.psum(gram, "help"),
        )
    held = partial
    mask = count // 2
    while mask >= 1:
        half = held.shape[1] // 2
        arrived = exchanged(jnp.concatenate([held[:, half:], gram], axis=1), "help", mask)
        held = held[:, :half] + arrived[:, :half]
        gram = gram + arrived[:, half:]
        mask //= 2
    return held, gram


def reduce_blk(gram):
    count = lax.axis_size("blk")
    if not is_power_of_two(count):
        return lax.psum(gram, "blk")
    mask = 1
    while mask < count:
        gram = gram + exchanged(gram, "blk", mask)
        mask *= 2
    return gram


def neighbour_panels(source):
    lowers = []
    uppers = []
    current = source
    for hop_index in range(BAND):
        current = shifted(current, "blk", 1)
        lowers.append(current)
    current = source
    for hop_index in range(BAND):
        current = shifted(current, "blk", -1)
        uppers.append(current)
    return lowers[::-1] + [source] + uppers


def local(vectors, tile_blocks, tile_row, tile_col, counts):
    groups = lax.axis_size("blk")
    piece_width = vectors.shape[1]
    group_width = piece_width * lax.axis_size("help")
    group_rows = group_width // TILE
    paired = groups % 2 == 0 and is_power_of_two(lax.axis_size("help"))
    tiles_per_piece = piece_width // TILE
    order = help_order()

    def placed(tile_index):
        return ((tile_index // tiles_per_piece) ^ order) * tiles_per_piece + tile_index % tiles_per_piece

    core = lax.axis_index("blk") % 2
    if paired:
        helpers = lax.axis_size("help")
        own_pair = jnp.concatenate([vectors, exchanged(vectors, "blk", 1)], axis=1)
        vectors, _ = lax.optimization_barrier((vectors, own_pair))
        own_pair = jnp.concatenate([own_pair, exchanged(own_pair, "help", 1)], axis=1)
        tile_row, tile_col, counts, _ = lax.optimization_barrier(
            (tile_row, tile_col, counts, own_pair)
        )
        mask = 2
        while mask < helpers:
            own_pair = jnp.concatenate([own_pair, exchanged(own_pair, "help", mask)], axis=1)
            mask *= 2
        crossing = [(b, b + 2) for b in range(0, groups - 2, 2)]
        crossing += [(b, b - 2) for b in range(3, groups, 2)]
        remote = lax.ppermute(own_pair, "blk", crossing)
        partner_remote = exchanged(remote, "blk", 1)
        sources = []
        for pair in (own_pair, remote, partner_remote):
            halves = pair.reshape(VEC, helpers, 2, piece_width)
            sources += [halves[:, :, side].reshape(VEC, group_width) for side in range(2)]
        full_panel = sources[0]
    else:
        full_panel = gather_help(vectors)
        sources = neighbour_panels(full_panel)
    slot_ids = jnp.arange(SLOTS, dtype=jnp.int32)[None, :]
    row_ids = jnp.arange(group_rows, dtype=jnp.int32)
    live = (slot_ids < counts[0][:, None]).astype(jnp.float32)
    column_place = placed(tile_col[0])
    row_place = placed(tile_row[0])
    one_hot = (row_place[:, :, None] == row_ids).astype(jnp.float32) * live[:, :, None]

    def batch_product(sources, panel_ids, first, last, step):
        stacked = jnp.stack(sources).reshape(len(sources), VEC, group_rows, TILE)
        stacked = stacked.transpose(0, 2, 1, 3)
        pieces = stacked[panel_ids[:, None], column_place[first:last:step]]
        contribution = jnp.einsum(
            "osit,ostu->osiu",
            pieces,
            tile_blocks[0, first:last:step],
            precision=lax.Precision.HIGH,
        )
        return jnp.einsum(
            "osiu,osr->iru",
            contribution,
            one_hot[first:last:step],
            precision=lax.Precision.HIGH,
        )

    if paired:
        panel_ids = jnp.where(
            core == 0,
            jnp.array([2, 3, 0, 1, 5], dtype=jnp.int32),
            jnp.array([5, 1, 0, 3, 2], dtype=jnp.int32),
        )
    else:
        panel_ids = jnp.arange(NOFF, dtype=jnp.int32)
    partial_value = batch_product(sources, panel_ids, 0, NOFF, 1)
    flattened = partial_value.reshape(VEC, group_width)
    basis_size = float(groups * group_width)
    correlation_term = jnp.dot(
        vectors, vectors.T, precision=lax.Precision.HIGHEST, preferred_element_type=jnp.float32
    )
    energy_term = jnp.dot(
        full_panel, flattened.T, precision=lax.Precision.HIGH, preferred_element_type=jnp.float32
    )
    gram = jnp.concatenate(
        [energy_term, correlation_term, jnp.zeros((VEC, GRAM_PAD - 2 * VEC), jnp.float32)], axis=1
    )
    product, gram = reduce_help(flattened, gram)
    gram = reduce_blk(gram)
    gram = gram / basis_size
    return (product, gram[:, :VEC], gram[:, VEC : 2 * VEC])


def solution(mesh):
    placed = (
        P(None, ("blk", "help")),
        P(("blk", "help"), None, None, None, None),
        P(("blk", "help"), None, None),
        P(("blk", "help"), None, None),
        P(("blk", "help"), None),
    )
    return jax.shard_map(
        local,
        mesh=mesh,
        in_specs=placed,
        out_specs=(P(None, ("blk", "help")), P(), P()),
        check_vma=False,
    )
```

```python
import jax
import jax.numpy as jnp
from jax import lax
from jax.sharding import PartitionSpec as P

VEC = 8
TILE = 256
BAND = 2
SLOTS = 3
NOFF = 5
GRAM_PAD = 128


def shifted(value, axis, steps):
    count = lax.axis_size(axis)
    initial, last = (max(0, -steps), min(count, count - steps))
    return lax.ppermute(value, axis, [(source, source + steps) for source in range(initial, last)])


def is_power_of_two(count):
    return count & (count - 1) == 0


def exchanged(value, axis, mask):
    count = lax.axis_size(axis)
    return lax.ppermute(value, axis, [(source, source ^ mask) for source in range(count)])


def help_order():
    count = lax.axis_size("help")
    if not is_power_of_two(count):
        return jnp.int32(0)
    return lax.axis_index("help").astype(jnp.int32)


def gather_help(piece):
    count = lax.axis_size("help")
    if not is_power_of_two(count):
        return lax.all_gather(piece, "help", axis=1, tiled=True)
    held = piece
    mask = 1
    while mask < count:
        held = jnp.concatenate([held, exchanged(held, "help", mask)], axis=1)
        mask *= 2
    return held


def reduce_help(partial, gram):
    count = lax.axis_size("help")
    if not is_power_of_two(count):
        return (
            lax.psum_scatter(partial, "help", scatter_dimension=1, tiled=True),
            lax.psum(gram, "help"),
        )
    held = partial
    mask = count // 2
    while mask >= 1:
        half = held.shape[1] // 2
        arrived = exchanged(jnp.concatenate([held[:, half:], gram], axis=1), "help", mask)
        held = held[:, :half] + arrived[:, :half]
        gram = gram + arrived[:, half:]
        mask //= 2
    return held, gram


def reduce_blk(gram):
    count = lax.axis_size("blk")
    if not is_power_of_two(count):
        return lax.psum(gram, "blk")
    mask = 1
    while mask < count:
        gram = gram + exchanged(gram, "blk", mask)
        mask *= 2
    return gram


def neighbour_panels(source):
    lowers = []
    uppers = []
    current = source
    for hop_index in range(BAND):
        current = shifted(current, "blk", 1)
        lowers.append(current)
    current = source
    for hop_index in range(BAND):
        current = shifted(current, "blk", -1)
        uppers.append(current)
    return lowers[::-1] + [source] + uppers


def local(vectors, tile_blocks, tile_row, tile_col, counts):
    groups = lax.axis_size("blk")
    piece_width = vectors.shape[1]
    group_width = piece_width * lax.axis_size("help")
    group_rows = group_width // TILE
    paired = groups % 2 == 0 and is_power_of_two(lax.axis_size("help"))
    tiles_per_piece = piece_width // TILE
    order = help_order()

    def placed(tile_index):
        return ((tile_index // tiles_per_piece) ^ order) * tiles_per_piece + tile_index % tiles_per_piece

    core = lax.axis_index("blk") % 2
    if paired:
        helpers = lax.axis_size("help")
        own_pair = jnp.concatenate([vectors, exchanged(vectors, "blk", 1)], axis=1)
        vectors, _ = lax.optimization_barrier((vectors, own_pair))
        own_pair = jnp.concatenate([own_pair, exchanged(own_pair, "help", 1)], axis=1)
        tile_row, tile_col, counts, _ = lax.optimization_barrier(
            (tile_row, tile_col, counts, own_pair)
        )
        mask = 2
        while mask < helpers:
            own_pair = jnp.concatenate([own_pair, exchanged(own_pair, "help", mask)], axis=1)
            mask *= 2
        core, _ = lax.optimization_barrier((core, own_pair))
        crossing = [(b, b + 2) for b in range(0, groups - 2, 2)]
        crossing += [(b, b - 2) for b in range(3, groups, 2)]
        remote = lax.ppermute(own_pair, "blk", crossing)
        partner_remote = exchanged(remote, "blk", 1)
        sources = []
        for pair in (own_pair, remote, partner_remote):
            halves = pair.reshape(VEC, helpers, 2, piece_width)
            sources += [halves[:, :, side].reshape(VEC, group_width) for side in range(2)]
        full_panel = sources[0]
    else:
        full_panel = gather_help(vectors)
        sources = neighbour_panels(full_panel)
    slot_ids = jnp.arange(SLOTS, dtype=jnp.int32)[None, :]
    row_ids = jnp.arange(group_rows, dtype=jnp.int32)
    live = (slot_ids < counts[0][:, None]).astype(jnp.float32)
    column_place = placed(tile_col[0])
    row_place = placed(tile_row[0])
    one_hot = (row_place[:, :, None] == row_ids).astype(jnp.float32) * live[:, :, None]

    def batch_product(sources, panel_ids, first, last, step):
        stacked = jnp.stack(sources).reshape(len(sources), VEC, group_rows, TILE)
        stacked = stacked.transpose(0, 2, 1, 3)
        pieces = stacked[panel_ids[:, None], column_place[first:last:step]]
        contribution = jnp.einsum(
            "osit,ostu->osiu",
            pieces,
            tile_blocks[0, first:last:step],
            precision=lax.Precision.HIGH,
        )
        return jnp.einsum(
            "osiu,osr->iru",
            contribution,
            one_hot[first:last:step],
            precision=lax.Precision.HIGH,
        )

    if paired:
        panel_ids = jnp.where(
            core == 0,
            jnp.array([2, 3, 0, 1, 5], dtype=jnp.int32),
            jnp.array([5, 1, 0, 3, 2], dtype=jnp.int32),
        )
    else:
        panel_ids = jnp.arange(NOFF, dtype=jnp.int32)
    partial_value = batch_product(sources, panel_ids, 0, NOFF, 1)
    flattened = partial_value.reshape(VEC, group_width)
    basis_size = float(groups * group_width)
    correlation_term = jnp.dot(
        vectors, vectors.T, precision=lax.Precision.HIGHEST, preferred_element_type=jnp.float32
    )
    energy_term = jnp.dot(
        full_panel, flattened.T, precision=lax.Precision.HIGH, preferred_element_type=jnp.float32
    )
    gram = jnp.concatenate(
        [energy_term, correlation_term, jnp.zeros((VEC, GRAM_PAD - 2 * VEC), jnp.float32)], axis=1
    )
    product, gram = reduce_help(flattened, gram)
    gram = reduce_blk(gram)
    gram = gram / basis_size
    return (product, gram[:, :VEC], gram[:, VEC : 2 * VEC])


def solution(mesh):
    placed = (
        P(None, ("blk", "help")),
        P(("blk", "help"), None, None, None, None),
        P(("blk", "help"), None, None),
        P(("blk", "help"), None, None),
        P(("blk", "help"), None),
    )
    return jax.shard_map(
        local,
        mesh=mesh,
        in_specs=placed,
        out_specs=(P(None, ("blk", "help")), P(), P()),
        check_vma=False,
    )
```

```python
import jax
import jax.numpy as jnp
from jax import lax
from jax.sharding import PartitionSpec as P

VEC = 8
TILE = 256
BAND = 2
SLOTS = 3
NOFF = 5
GRAM_PAD = 128


def shifted(value, axis, steps):
    count = lax.axis_size(axis)
    initial, last = (max(0, -steps), min(count, count - steps))
    return lax.ppermute(value, axis, [(source, source + steps) for source in range(initial, last)])


def is_power_of_two(count):
    return count & (count - 1) == 0


def exchanged(value, axis, mask):
    count = lax.axis_size(axis)
    return lax.ppermute(value, axis, [(source, source ^ mask) for source in range(count)])


def help_order():
    count = lax.axis_size("help")
    if not is_power_of_two(count):
        return jnp.int32(0)
    return lax.axis_index("help").astype(jnp.int32)


def gather_help(piece):
    count = lax.axis_size("help")
    if not is_power_of_two(count):
        return lax.all_gather(piece, "help", axis=1, tiled=True)
    held = piece
    mask = 1
    while mask < count:
        held = jnp.concatenate([held, exchanged(held, "help", mask)], axis=1)
        mask *= 2
    return held


def reduce_help(partial, gram):
    count = lax.axis_size("help")
    if not is_power_of_two(count):
        return (
            lax.psum_scatter(partial, "help", scatter_dimension=1, tiled=True),
            lax.psum(gram, "help"),
        )
    held = partial
    mask = count // 2
    while mask >= 1:
        half = held.shape[1] // 2
        arrived = exchanged(jnp.concatenate([held[:, half:], gram], axis=1), "help", mask)
        held = held[:, :half] + arrived[:, :half]
        gram = gram + arrived[:, half:]
        mask //= 2
    return held, gram


def reduce_blk(gram):
    count = lax.axis_size("blk")
    if not is_power_of_two(count):
        return lax.psum(gram, "blk")
    mask = 1
    while mask < count:
        gram = gram + exchanged(gram, "blk", mask)
        mask *= 2
    return gram


def neighbour_panels(source):
    lowers = []
    uppers = []
    current = source
    for hop_index in range(BAND):
        current = shifted(current, "blk", 1)
        lowers.append(current)
    current = source
    for hop_index in range(BAND):
        current = shifted(current, "blk", -1)
        uppers.append(current)
    return lowers[::-1] + [source] + uppers


def local(vectors, tile_blocks, tile_row, tile_col, counts):
    groups = lax.axis_size("blk")
    piece_width = vectors.shape[1]
    group_width = piece_width * lax.axis_size("help")
    group_rows = group_width // TILE
    paired = groups % 2 == 0 and is_power_of_two(lax.axis_size("help"))
    tiles_per_piece = piece_width // TILE
    order = help_order()

    def placed(tile_index):
        return ((tile_index // tiles_per_piece) ^ order) * tiles_per_piece + tile_index % tiles_per_piece

    core = lax.axis_index("blk") % 2
    if paired:
        helpers = lax.axis_size("help")
        own_pair = jnp.concatenate([vectors, exchanged(vectors, "blk", 1)], axis=1)
        vectors, _ = lax.optimization_barrier((vectors, own_pair))
        own_pair = jnp.concatenate([own_pair, exchanged(own_pair, "help", 1)], axis=1)
        tile_row, tile_col, counts, _ = lax.optimization_barrier(
            (tile_row, tile_col, counts, own_pair)
        )
        mask = 2
        while mask < helpers:
            own_pair = jnp.concatenate([own_pair, exchanged(own_pair, "help", mask)], axis=1)
            mask *= 2
        core, _ = lax.optimization_barrier((core, own_pair))
        crossing = [(b, b + 2) for b in range(0, groups - 2, 2)]
        crossing += [(b, b - 2) for b in range(3, groups, 2)]
        remote = lax.ppermute(own_pair, "blk", crossing)
        partner_remote = exchanged(remote, "blk", 1)
        sources = []
        for pair in (own_pair, remote, partner_remote):
            halves = pair.reshape(VEC, helpers, 2, piece_width)
            sources += [halves[:, :, side].reshape(VEC, group_width) for side in range(2)]
        full_panel = sources[0]
    else:
        full_panel = gather_help(vectors)
        sources = neighbour_panels(full_panel)
    slot_ids = jnp.arange(SLOTS, dtype=jnp.int32)[None, :]
    row_ids = jnp.arange(group_rows, dtype=jnp.int32)
    live = (slot_ids < counts[0][:, None]).astype(jnp.float32)
    column_place = placed(tile_col[0])
    row_place = placed(tile_row[0])
    one_hot = (row_place[:, :, None] == row_ids).astype(jnp.float32) * live[:, :, None]

    def batch_product(sources, panel_ids, first, last, step):
        stacked = jnp.stack(sources).reshape(len(sources), VEC, group_rows, TILE)
        stacked = stacked.transpose(0, 2, 1, 3)
        pieces = stacked[panel_ids[:, None], column_place[first:last:step]]
        contribution = jnp.einsum(
            "osit,ostu->osiu",
            pieces,
            tile_blocks[0, first:last:step],
            precision=lax.Precision.HIGH,
        )
        return jnp.einsum(
            "osiu,osr->iru",
            contribution,
            one_hot[first:last:step],
            precision=lax.Precision.HIGH,
        )

    if paired:
        panel_ids = jnp.where(
            core == 0,
            jnp.array([2, 3, 0, 1, 5], dtype=jnp.int32),
            jnp.array([5, 1, 0, 3, 2], dtype=jnp.int32),
        )
    else:
        panel_ids = jnp.arange(NOFF, dtype=jnp.int32)
    partial_value = batch_product(sources, panel_ids, 0, NOFF, 1)
    flattened = partial_value.reshape(VEC, group_width)
    basis_size = float(groups * group_width)
    correlation_term = jnp.dot(
        vectors, vectors.T, precision=lax.Precision.HIGHEST, preferred_element_type=jnp.float32
    )
    energy_term = jnp.dot(
        full_panel, flattened.T, precision=lax.Precision.HIGH, preferred_element_type=jnp.float32
    )
    gram = jnp.concatenate(
        [energy_term, correlation_term, jnp.zeros((VEC, GRAM_PAD - 2 * VEC), jnp.float32)], axis=1
    )
    exact_scale = is_power_of_two(groups * group_width)
    if exact_scale:
        gram = gram / basis_size
    product, gram = reduce_help(flattened, gram)
    gram = reduce_blk(gram)
    if not exact_scale:
        gram = gram / basis_size
    return (product, gram[:, :VEC], gram[:, VEC : 2 * VEC])


def solution(mesh):
    placed = (
        P(None, ("blk", "help")),
        P(("blk", "help"), None, None, None, None),
        P(("blk", "help"), None, None),
        P(("blk", "help"), None, None),
        P(("blk", "help"), None),
    )
    return jax.shard_map(
        local,
        mesh=mesh,
        in_specs=placed,
        out_specs=(P(None, ("blk", "help")), P(), P()),
        check_vma=False,
    )
```

```python
import jax
import jax.numpy as jnp
from jax import lax
from jax.sharding import PartitionSpec as P

VEC = 8
TILE = 256
BAND = 2
SLOTS = 3
NOFF = 5
GRAM_PAD = 128


def shifted(value, axis, steps):
    count = lax.axis_size(axis)
    initial, last = (max(0, -steps), min(count, count - steps))
    return lax.ppermute(value, axis, [(source, source + steps) for source in range(initial, last)])


def is_power_of_two(count):
    return count & (count - 1) == 0


def exchanged(value, axis, mask):
    count = lax.axis_size(axis)
    return lax.ppermute(value, axis, [(source, source ^ mask) for source in range(count)])


def help_order():
    count = lax.axis_size("help")
    if not is_power_of_two(count):
        return jnp.int32(0)
    return lax.axis_index("help").astype(jnp.int32)


def gather_help(piece):
    count = lax.axis_size("help")
    if not is_power_of_two(count):
        return lax.all_gather(piece, "help", axis=1, tiled=True)
    held = piece
    mask = 1
    while mask < count:
        held = jnp.concatenate([held, exchanged(held, "help", mask)], axis=1)
        mask *= 2
    return held


def reduce_help(partial, gram):
    count = lax.axis_size("help")
    if not is_power_of_two(count):
        return (
            lax.psum_scatter(partial, "help", scatter_dimension=1, tiled=True),
            lax.psum(gram, "help"),
        )
    held = partial
    mask = count // 2
    while mask >= 1:
        half = held.shape[1] // 2
        arrived = exchanged(jnp.concatenate([held[:, half:], gram], axis=1), "help", mask)
        held = held[:, :half] + arrived[:, :half]
        gram = gram + arrived[:, half:]
        mask //= 2
    return held, gram


def reduce_blk(gram):
    count = lax.axis_size("blk")
    if not is_power_of_two(count):
        return lax.psum(gram, "blk")
    mask = 1
    while mask < count:
        gram = gram + exchanged(gram, "blk", mask)
        mask *= 2
    return gram


def neighbour_panels(source):
    lowers = []
    uppers = []
    current = source
    for hop_index in range(BAND):
        current = shifted(current, "blk", 1)
        lowers.append(current)
    current = source
    for hop_index in range(BAND):
        current = shifted(current, "blk", -1)
        uppers.append(current)
    return lowers[::-1] + [source] + uppers


def local(vectors, tile_blocks, tile_row, tile_col, counts):
    groups = lax.axis_size("blk")
    piece_width = vectors.shape[1]
    group_width = piece_width * lax.axis_size("help")
    group_rows = group_width // TILE
    paired = groups % 2 == 0 and lax.axis_size("help") > 1 and is_power_of_two(lax.axis_size("help"))
    tiles_per_piece = piece_width // TILE
    order = help_order()

    def placed(tile_index):
        return ((tile_index // tiles_per_piece) ^ order) * tiles_per_piece + tile_index % tiles_per_piece

    core = lax.axis_index("blk") % 2
    if paired:
        helpers = lax.axis_size("help")
        own_pair = jnp.concatenate([vectors, exchanged(vectors, "help", 1)], axis=1)
        vectors, _ = lax.optimization_barrier((vectors, own_pair))
        own_pair = jnp.concatenate([own_pair, exchanged(own_pair, "blk", 1)], axis=1)
        tile_row, tile_col, counts, _ = lax.optimization_barrier(
            (tile_row, tile_col, counts, own_pair)
        )
        mask = 2
        while mask < helpers:
            own_pair = jnp.concatenate([own_pair, exchanged(own_pair, "help", mask)], axis=1)
            mask *= 2
        core, _ = lax.optimization_barrier((core, own_pair))
        crossing = [(b, b + 2) for b in range(0, groups - 2, 2)]
        crossing += [(b, b - 2) for b in range(3, groups, 2)]
        remote = lax.ppermute(own_pair, "blk", crossing)
        partner_remote = exchanged(remote, "blk", 1)
        sources = []
        for pair in (own_pair, remote, partner_remote):
            halves = pair.reshape(VEC, helpers // 2, 2, 2 * piece_width)
            sources += [halves[:, :, side].reshape(VEC, group_width) for side in range(2)]
        full_panel = sources[0]
    else:
        full_panel = gather_help(vectors)
        sources = neighbour_panels(full_panel)
    slot_ids = jnp.arange(SLOTS, dtype=jnp.int32)[None, :]
    row_ids = jnp.arange(group_rows, dtype=jnp.int32)
    live = (slot_ids < counts[0][:, None]).astype(jnp.float32)
    column_place = placed(tile_col[0])
    row_place = placed(tile_row[0])
    one_hot = (row_place[:, :, None] == row_ids).astype(jnp.float32) * live[:, :, None]

    def batch_product(sources, panel_ids, first, last, step):
        stacked = jnp.stack(sources).reshape(len(sources), VEC, group_rows, TILE)
        stacked = stacked.transpose(0, 2, 1, 3)
        pieces = stacked[panel_ids[:, None], column_place[first:last:step]]
        contribution = jnp.einsum(
            "osit,ostu->osiu",
            pieces,
            tile_blocks[0, first:last:step],
            precision=lax.Precision.HIGH,
        )
        return jnp.einsum(
            "osiu,osr->iru",
            contribution,
            one_hot[first:last:step],
            precision=lax.Precision.HIGH,
        )

    if paired:
        panel_ids = jnp.where(
            core == 0,
            jnp.array([2, 3, 0, 1, 5], dtype=jnp.int32),
            jnp.array([5, 1, 0, 3, 2], dtype=jnp.int32),
        )
    else:
        panel_ids = jnp.arange(NOFF, dtype=jnp.int32)
    partial_value = batch_product(sources, panel_ids, 0, NOFF, 1)
    flattened = partial_value.reshape(VEC, group_width)
    basis_size = float(groups * group_width)
    correlation_term = jnp.dot(
        vectors, vectors.T, precision=lax.Precision.HIGHEST, preferred_element_type=jnp.float32
    )
    energy_term = jnp.dot(
        full_panel, flattened.T, precision=lax.Precision.HIGH, preferred_element_type=jnp.float32
    )
    gram = jnp.concatenate(
        [energy_term, correlation_term, jnp.zeros((VEC, GRAM_PAD - 2 * VEC), jnp.float32)], axis=1
    )
    exact_scale = is_power_of_two(groups * group_width)
    if exact_scale:
        gram = gram / basis_size
    product, gram = reduce_help(flattened, gram)
    gram = reduce_blk(gram)
    if not exact_scale:
        gram = gram / basis_size
    return (product, gram[:, :VEC], gram[:, VEC : 2 * VEC])


def solution(mesh):
    placed = (
        P(None, ("blk", "help")),
        P(("blk", "help"), None, None, None, None),
        P(("blk", "help"), None, None),
        P(("blk", "help"), None, None),
        P(("blk", "help"), None),
    )
    return jax.shard_map(
        local,
        mesh=mesh,
        in_specs=placed,
        out_specs=(P(None, ("blk", "help")), P(), P()),
        check_vma=False,
    )
```

```python
import jax
import jax.numpy as jnp
from jax import lax
from jax.sharding import PartitionSpec as P

VEC = 8
TILE = 256
BAND = 2
SLOTS = 3
NOFF = 5
GRAM_PAD = 128


def shifted(value, axis, steps):
    count = lax.axis_size(axis)
    initial, last = (max(0, -steps), min(count, count - steps))
    return lax.ppermute(value, axis, [(source, source + steps) for source in range(initial, last)])


def is_power_of_two(count):
    return count & (count - 1) == 0


def exchanged(value, axis, mask):
    count = lax.axis_size(axis)
    return lax.ppermute(value, axis, [(source, source ^ mask) for source in range(count)])


def help_order():
    count = lax.axis_size("help")
    if not is_power_of_two(count):
        return jnp.int32(0)
    return lax.axis_index("help").astype(jnp.int32)


def gather_help(piece):
    count = lax.axis_size("help")
    if not is_power_of_two(count):
        return lax.all_gather(piece, "help", axis=1, tiled=True)
    held = piece
    mask = 1
    while mask < count:
        held = jnp.concatenate([held, exchanged(held, "help", mask)], axis=1)
        mask *= 2
    return held


def reduce_help(partial, gram):
    count = lax.axis_size("help")
    if not is_power_of_two(count):
        return (
            lax.psum_scatter(partial, "help", scatter_dimension=1, tiled=True),
            lax.psum(gram, "help"),
        )
    held = partial
    mask = count // 2
    while mask >= 1:
        half = held.shape[1] // 2
        arrived = exchanged(jnp.concatenate([held[:, half:], gram], axis=1), "help", mask)
        held = held[:, :half] + arrived[:, :half]
        gram = gram + arrived[:, half:]
        mask //= 2
    return held, gram


def reduce_blk(gram):
    count = lax.axis_size("blk")
    if not is_power_of_two(count):
        return lax.psum(gram, "blk")
    mask = 1
    while mask < count:
        gram = gram + exchanged(gram, "blk", mask)
        mask *= 2
    return gram


def neighbour_panels(source):
    lowers = []
    uppers = []
    current = source
    for hop_index in range(BAND):
        current = shifted(current, "blk", 1)
        lowers.append(current)
    current = source
    for hop_index in range(BAND):
        current = shifted(current, "blk", -1)
        uppers.append(current)
    return lowers[::-1] + [source] + uppers


def local(vectors, tile_blocks, tile_row, tile_col, counts):
    groups = lax.axis_size("blk")
    piece_width = vectors.shape[1]
    group_width = piece_width * lax.axis_size("help")
    group_rows = group_width // TILE
    paired = groups % 2 == 0 and lax.axis_size("help") > 1 and is_power_of_two(lax.axis_size("help"))
    tiles_per_piece = piece_width // TILE
    order = help_order()

    def placed(tile_index):
        return ((tile_index // tiles_per_piece) ^ order) * tiles_per_piece + tile_index % tiles_per_piece

    core = lax.axis_index("blk") % 2
    if paired:
        helpers = lax.axis_size("help")
        own_pair = jnp.concatenate([vectors, exchanged(vectors, "help", 1)], axis=1)
        own_pair = jnp.concatenate([own_pair, exchanged(own_pair, "blk", 1)], axis=1)
        tile_row, tile_col, counts, vectors, _ = lax.optimization_barrier(
            (tile_row, tile_col, counts, vectors, own_pair)
        )
        mask = 2
        while mask < helpers:
            own_pair = jnp.concatenate([own_pair, exchanged(own_pair, "help", mask)], axis=1)
            mask *= 2
        core, _ = lax.optimization_barrier((core, own_pair))
        crossing = [(b, b + 2) for b in range(0, groups - 2, 2)]
        crossing += [(b, b - 2) for b in range(3, groups, 2)]
        remote = lax.ppermute(own_pair, "blk", crossing)
        partner_remote = exchanged(remote, "blk", 1)
        sources = []
        for pair in (own_pair, remote, partner_remote):
            halves = pair.reshape(VEC, helpers // 2, 2, 2 * piece_width)
            sources += [halves[:, :, side].reshape(VEC, group_width) for side in range(2)]
        full_panel = sources[0]
    else:
        full_panel = gather_help(vectors)
        sources = neighbour_panels(full_panel)
    slot_ids = jnp.arange(SLOTS, dtype=jnp.int32)[None, :]
    row_ids = jnp.arange(group_rows, dtype=jnp.int32)
    live = (slot_ids < counts[0][:, None]).astype(jnp.float32)
    column_place = placed(tile_col[0])
    row_place = placed(tile_row[0])
    one_hot = (row_place[:, :, None] == row_ids).astype(jnp.float32) * live[:, :, None]

    def batch_product(sources, panel_ids, first, last, step):
        stacked = jnp.stack(sources).reshape(len(sources), VEC, group_rows, TILE)
        stacked = stacked.transpose(0, 2, 1, 3)
        pieces = stacked[panel_ids[:, None], column_place[first:last:step]]
        contribution = jnp.einsum(
            "osit,ostu->osiu",
            pieces,
            tile_blocks[0, first:last:step],
            precision=lax.Precision.HIGH,
        )
        return jnp.einsum(
            "osiu,osr->iru",
            contribution,
            one_hot[first:last:step],
            precision=lax.Precision.HIGH,
        )

    if paired:
        panel_ids = jnp.where(
            core == 0,
            jnp.array([2, 3, 0, 1, 5], dtype=jnp.int32),
            jnp.array([5, 1, 0, 3, 2], dtype=jnp.int32),
        )
    else:
        panel_ids = jnp.arange(NOFF, dtype=jnp.int32)
    partial_value = batch_product(sources, panel_ids, 0, NOFF, 1)
    flattened = partial_value.reshape(VEC, group_width)
    basis_size = float(groups * group_width)
    correlation_term = jnp.dot(
        vectors, vectors.T, precision=lax.Precision.HIGHEST, preferred_element_type=jnp.float32
    )
    energy_term = jnp.dot(
        full_panel, flattened.T, precision=lax.Precision.HIGH, preferred_element_type=jnp.float32
    )
    gram = jnp.concatenate(
        [energy_term, correlation_term, jnp.zeros((VEC, GRAM_PAD - 2 * VEC), jnp.float32)], axis=1
    )
    exact_scale = is_power_of_two(groups * group_width)
    if exact_scale:
        gram = gram / basis_size
    product, gram = reduce_help(flattened, gram)
    gram = reduce_blk(gram)
    if not exact_scale:
        gram = gram / basis_size
    return (product, gram[:, :VEC], gram[:, VEC : 2 * VEC])


def solution(mesh):
    placed = (
        P(None, ("blk", "help")),
        P(("blk", "help"), None, None, None, None),
        P(("blk", "help"), None, None),
        P(("blk", "help"), None, None),
        P(("blk", "help"), None),
    )
    return jax.shard_map(
        local,
        mesh=mesh,
        in_specs=placed,
        out_specs=(P(None, ("blk", "help")), P(), P()),
        check_vma=False,
    )
```

```python
import jax
import jax.numpy as jnp
from jax import lax
from jax.sharding import PartitionSpec as P

VEC = 8
TILE = 256
BAND = 2
SLOTS = 3
NOFF = 5
GRAM_PAD = 128


def shifted(value, axis, steps):
    count = lax.axis_size(axis)
    initial, last = (max(0, -steps), min(count, count - steps))
    return lax.ppermute(value, axis, [(source, source + steps) for source in range(initial, last)])


def is_power_of_two(count):
    return count & (count - 1) == 0


def exchanged(value, axis, mask):
    count = lax.axis_size(axis)
    return lax.ppermute(value, axis, [(source, source ^ mask) for source in range(count)])


def help_order():
    count = lax.axis_size("help")
    if not is_power_of_two(count):
        return jnp.int32(0)
    return lax.axis_index("help").astype(jnp.int32)


def gather_help(piece):
    count = lax.axis_size("help")
    if not is_power_of_two(count):
        return lax.all_gather(piece, "help", axis=1, tiled=True)
    held = piece
    mask = 1
    while mask < count:
        held = jnp.concatenate([held, exchanged(held, "help", mask)], axis=1)
        mask *= 2
    return held


def reduce_help(partial, gram):
    count = lax.axis_size("help")
    if not is_power_of_two(count):
        return (
            lax.psum_scatter(partial, "help", scatter_dimension=1, tiled=True),
            lax.psum(gram, "help"),
        )
    held = partial
    mask = count // 2
    while mask >= 1:
        half = held.shape[1] // 2
        arrived = exchanged(jnp.concatenate([held[:, half:], gram], axis=1), "help", mask)
        held = held[:, :half] + arrived[:, :half]
        gram = gram + arrived[:, half:]
        mask //= 2
    return held, gram


def reduce_blk(gram):
    count = lax.axis_size("blk")
    if not is_power_of_two(count):
        return lax.psum(gram, "blk")
    mask = 1
    while mask < count:
        gram = gram + exchanged(gram, "blk", mask)
        mask *= 2
    return gram


def neighbour_panels(source):
    lowers = []
    uppers = []
    current = source
    for hop_index in range(BAND):
        current = shifted(current, "blk", 1)
        lowers.append(current)
    current = source
    for hop_index in range(BAND):
        current = shifted(current, "blk", -1)
        uppers.append(current)
    return lowers[::-1] + [source] + uppers


def local(vectors, tile_blocks, tile_row, tile_col, counts):
    groups = lax.axis_size("blk")
    piece_width = vectors.shape[1]
    group_width = piece_width * lax.axis_size("help")
    group_rows = group_width // TILE
    paired = groups % 2 == 0 and lax.axis_size("help") > 1 and is_power_of_two(lax.axis_size("help"))
    tiles_per_piece = piece_width // TILE
    order = help_order()

    def placed(tile_index):
        return ((tile_index // tiles_per_piece) ^ order) * tiles_per_piece + tile_index % tiles_per_piece

    core = lax.axis_index("blk") % 2
    if paired:
        helpers = lax.axis_size("help")
        own_pair = jnp.concatenate([vectors, exchanged(vectors, "help", 1)], axis=1)
        own_pair = jnp.concatenate([own_pair, exchanged(own_pair, "blk", 1)], axis=1)
        tile_row, tile_col, counts, _ = lax.optimization_barrier(
            (tile_row, tile_col, counts, own_pair)
        )
        mask = 2
        while mask < helpers:
            own_pair = jnp.concatenate([own_pair, exchanged(own_pair, "help", mask)], axis=1)
            mask *= 2
        core, _ = lax.optimization_barrier((core, own_pair))
        crossing = [(b, b + 2) for b in range(0, groups - 2, 2)]
        crossing += [(b, b - 2) for b in range(3, groups, 2)]
        remote = lax.ppermute(own_pair, "blk", crossing)
        partner_remote = exchanged(remote, "blk", 1)
        sources = []
        for pair in (own_pair, remote, partner_remote):
            halves = pair.reshape(VEC, helpers // 2, 2, 2 * piece_width)
            sources += [halves[:, :, side].reshape(VEC, group_width) for side in range(2)]
        full_panel = sources[0]
    else:
        full_panel = gather_help(vectors)
        sources = neighbour_panels(full_panel)
    slot_ids = jnp.arange(SLOTS, dtype=jnp.int32)[None, :]
    row_ids = jnp.arange(group_rows, dtype=jnp.int32)
    live = (slot_ids < counts[0][:, None]).astype(jnp.float32)
    column_place = placed(tile_col[0])
    row_place = placed(tile_row[0])
    one_hot = (row_place[:, :, None] == row_ids).astype(jnp.float32) * live[:, :, None]

    def batch_product(sources, panel_ids, first, last, step):
        stacked = jnp.stack(sources).reshape(len(sources), VEC, group_rows, TILE)
        stacked = stacked.transpose(0, 2, 1, 3)
        pieces = stacked[panel_ids[:, None], column_place[first:last:step]]
        contribution = jnp.einsum(
            "osit,ostu->osiu",
            pieces,
            tile_blocks[0, first:last:step],
            precision=lax.Precision.HIGH,
        )
        return jnp.einsum(
            "osiu,osr->iru",
            contribution,
            one_hot[first:last:step],
            precision=lax.Precision.HIGH,
        )

    if paired:
        panel_ids = jnp.where(
            core == 0,
            jnp.array([2, 3, 0, 1, 5], dtype=jnp.int32),
            jnp.array([5, 1, 0, 3, 2], dtype=jnp.int32),
        )
    else:
        panel_ids = jnp.arange(NOFF, dtype=jnp.int32)
    partial_value = batch_product(sources, panel_ids, 0, NOFF, 1)
    flattened = partial_value.reshape(VEC, group_width)
    basis_size = float(groups * group_width)
    correlation_term = jnp.dot(
        vectors, vectors.T, precision=lax.Precision.HIGHEST, preferred_element_type=jnp.float32
    )
    energy_term = jnp.dot(
        full_panel, flattened.T, precision=lax.Precision.HIGH, preferred_element_type=jnp.float32
    )
    gram = jnp.concatenate(
        [energy_term, correlation_term, jnp.zeros((VEC, GRAM_PAD - 2 * VEC), jnp.float32)], axis=1
    )
    exact_scale = is_power_of_two(groups * group_width)
    if exact_scale:
        gram = gram / basis_size
    product, gram = reduce_help(flattened, gram)
    gram = reduce_blk(gram)
    if not exact_scale:
        gram = gram / basis_size
    return (product, gram[:, :VEC], gram[:, VEC : 2 * VEC])


def solution(mesh):
    placed = (
        P(None, ("blk", "help")),
        P(("blk", "help"), None, None, None, None),
        P(("blk", "help"), None, None),
        P(("blk", "help"), None, None),
        P(("blk", "help"), None),
    )
    return jax.shard_map(
        local,
        mesh=mesh,
        in_specs=placed,
        out_specs=(P(None, ("blk", "help")), P(), P()),
        check_vma=False,
    )
```

```python
import jax
import jax.numpy as jnp
from jax import lax
from jax.sharding import PartitionSpec as P

VEC = 8
TILE = 256
BAND = 2
SLOTS = 3
NOFF = 5
GRAM_PAD = 128


def shifted(value, axis, steps):
    count = lax.axis_size(axis)
    initial, last = (max(0, -steps), min(count, count - steps))
    return lax.ppermute(value, axis, [(source, source + steps) for source in range(initial, last)])


def is_power_of_two(count):
    return count & (count - 1) == 0


def exchanged(value, axis, mask):
    count = lax.axis_size(axis)
    return lax.ppermute(value, axis, [(source, source ^ mask) for source in range(count)])


def help_order():
    count = lax.axis_size("help")
    if not is_power_of_two(count):
        return jnp.int32(0)
    return lax.axis_index("help").astype(jnp.int32)


def gather_help(piece):
    count = lax.axis_size("help")
    if not is_power_of_two(count):
        return lax.all_gather(piece, "help", axis=1, tiled=True)
    held = piece
    mask = 1
    while mask < count:
        held = jnp.concatenate([held, exchanged(held, "help", mask)], axis=1)
        mask *= 2
    return held


def reduce_help(partial, gram):
    count = lax.axis_size("help")
    if not is_power_of_two(count):
        return (
            lax.psum_scatter(partial, "help", scatter_dimension=1, tiled=True),
            lax.psum(gram, "help"),
        )
    held = partial
    mask = count // 2
    while mask >= 1:
        half = held.shape[1] // 2
        arrived = exchanged(jnp.concatenate([held[:, half:], gram], axis=1), "help", mask)
        held = held[:, :half] + arrived[:, :half]
        gram = gram + arrived[:, half:]
        mask //= 2
    return held, gram


def reduce_blk(gram):
    count = lax.axis_size("blk")
    if not is_power_of_two(count):
        return lax.psum(gram, "blk")
    mask = 1
    while mask < count:
        gram = gram + exchanged(gram, "blk", mask)
        mask *= 2
    return gram


def neighbour_panels(source):
    lowers = []
    uppers = []
    current = source
    for hop_index in range(BAND):
        current = shifted(current, "blk", 1)
        lowers.append(current)
    current = source
    for hop_index in range(BAND):
        current = shifted(current, "blk", -1)
        uppers.append(current)
    return lowers[::-1] + [source] + uppers


def local(vectors, tile_blocks, tile_row, tile_col, counts):
    groups = lax.axis_size("blk")
    piece_width = vectors.shape[1]
    group_width = piece_width * lax.axis_size("help")
    group_rows = group_width // TILE
    paired = groups % 2 == 0 and lax.axis_size("help") > 1 and is_power_of_two(lax.axis_size("help"))
    tiles_per_piece = piece_width // TILE
    order = help_order()

    def placed(tile_index):
        return ((tile_index // tiles_per_piece) ^ order) * tiles_per_piece + tile_index % tiles_per_piece

    core = lax.axis_index("blk") % 2
    if paired:
        helpers = lax.axis_size("help")
        own_pair = jnp.concatenate([vectors, exchanged(vectors, "help", 1)], axis=1)
        vectors, _ = lax.optimization_barrier((vectors, own_pair))
        own_pair = jnp.concatenate([own_pair, exchanged(own_pair, "blk", 1)], axis=1)
        tile_row, tile_col, counts, _ = lax.optimization_barrier(
            (tile_row, tile_col, counts, own_pair)
        )
        mask = 2
        while mask < helpers:
            own_pair = jnp.concatenate([own_pair, exchanged(own_pair, "help", mask)], axis=1)
            mask *= 2
        core, _ = lax.optimization_barrier((core, own_pair))
        crossing = [(b, b + 2) for b in range(0, groups - 2, 2)]
        crossing += [(b, b - 2) for b in range(3, groups, 2)]
        remote = lax.ppermute(own_pair, "blk", crossing)
        partner_remote = exchanged(remote, "blk", 1)
        sources = []
        for pair in (own_pair, remote, partner_remote):
            halves = pair.reshape(VEC, helpers // 2, 2, 2 * piece_width)
            sources += [halves[:, :, side].reshape(VEC, group_width) for side in range(2)]
        full_panel = sources[0]
    else:
        full_panel = gather_help(vectors)
        sources = neighbour_panels(full_panel)
    slot_ids = jnp.arange(SLOTS, dtype=jnp.int32)[None, :]
    row_ids = jnp.arange(group_rows, dtype=jnp.int32)
    live = (slot_ids < counts[0][:, None]).astype(jnp.float32)
    column_place = placed(tile_col[0])
    row_place = placed(tile_row[0])
    one_hot = (row_place[:, :, None] == row_ids).astype(jnp.float32) * live[:, :, None]

    def batch_product(sources, panel_ids, first, last, step):
        stacked = jnp.stack(sources).reshape(len(sources), VEC, group_rows, TILE)
        stacked = stacked.transpose(0, 2, 1, 3)
        pieces = stacked[panel_ids[:, None], column_place[first:last:step]]
        contribution = jnp.einsum(
            "osit,ostu->osiu",
            pieces,
            tile_blocks[0, first:last:step],
            precision=lax.Precision.HIGH,
        )
        placed_rows = row_place[first:last:step].reshape(-1)
        weighted = contribution * live[first:last:step][:, :, None, None]
        rows = jnp.zeros((group_rows, VEC, TILE), jnp.float32)
        rows = rows.at[placed_rows].add(weighted.reshape(-1, VEC, TILE))
        return rows.transpose(1, 0, 2)

    if paired:
        panel_ids = jnp.where(
            core == 0,
            jnp.array([2, 3, 0, 1, 5], dtype=jnp.int32),
            jnp.array([5, 1, 0, 3, 2], dtype=jnp.int32),
        )
    else:
        panel_ids = jnp.arange(NOFF, dtype=jnp.int32)
    partial_value = batch_product(sources, panel_ids, 0, NOFF, 1)
    flattened = partial_value.reshape(VEC, group_width)
    basis_size = float(groups * group_width)
    correlation_term = jnp.dot(
        vectors, vectors.T, precision=lax.Precision.HIGHEST, preferred_element_type=jnp.float32
    )
    energy_term = jnp.dot(
        full_panel, flattened.T, precision=lax.Precision.HIGH, preferred_element_type=jnp.float32
    )
    gram = jnp.concatenate(
        [energy_term, correlation_term, jnp.zeros((VEC, GRAM_PAD - 2 * VEC), jnp.float32)], axis=1
    )
    exact_scale = is_power_of_two(groups * group_width)
    if exact_scale:
        gram = gram / basis_size
    product, gram = reduce_help(flattened, gram)
    gram = reduce_blk(gram)
    if not exact_scale:
        gram = gram / basis_size
    return (product, gram[:, :VEC], gram[:, VEC : 2 * VEC])


def solution(mesh):
    placed = (
        P(None, ("blk", "help")),
        P(("blk", "help"), None, None, None, None),
        P(("blk", "help"), None, None),
        P(("blk", "help"), None, None),
        P(("blk", "help"), None),
    )
    return jax.shard_map(
        local,
        mesh=mesh,
        in_specs=placed,
        out_specs=(P(None, ("blk", "help")), P(), P()),
        check_vma=False,
    )
```
